128 devices in a mesh: tm: 64 (over x, z, y_lo, core), row: 2 (over y_hi).
Axes of the slice: x: 4, y: 4 (y_hi: 2, y_lo: 2; y = y_hi * 2 + y_lo), z: 4, core: 2. Of those that a mesh axis runs over, the one named last changes fastest.
Arguments:
- slice_ops: bfloat16 [64, 2048, 2048], P('tm', 'row'), may hold values from -6 to 6
- base_op: bfloat16 [2048, 2048], replicated, may hold values from -6 to 6
- load_table: float32 [16, 2048], replicated, may hold values from -1 to 1
- phase_idx: int32 [64, 2], P('tm'), may hold values from 0 to 15
- step_counts: int32 [64, 2], P('tm'), may hold values from 1 to 8
Outputs:
- windows: bfloat16 [64, 2048, 2048], P('tm', 'row')
The draws below stay inside these ranges and needn't reach their ends.
All inputs are finite; a program needn't handle non-finite values.
Results may differ from the reference program's by a relative error of at most 0.012.
Values may be sent and summed in bfloat16 or wider, within the bound.
No kernel may reach another device: no remote copies, remote signals or barrier semaphores. Data moves between devices by JAX's collectives and lax.ppermute only.
A program may use at most 128 MiB of HBM per device.

```python
import math
import jax
import jax.numpy as jnp
from jax import lax

S = 2048
PHASES = 16
SUB = 2
LEVELS = 2
SLICES = 64


def plant(result, key, least, top_value):
    shape = result.shape
    index_at = [jax.random.randint(jax.random.fold_in(key, axis), (), 0, shape[axis]) for axis in range(len(shape))]
    result = result.at[tuple(index_at)].set(least)
    longest = shape.index(max(shape))
    index_at[longest] = (index_at[longest] + 1) % shape[longest]
    return result.at[tuple(index_at)].set(top_value)


def level_of(stream_key, extent, pieces, low, top_value):
    loudness = 1.0
    for dim, shards_of in pieces:
        draws = jax.random.uniform(jax.random.fold_in(jax.random.fold_in(stream_key, 6), dim), (shards_of,), jnp.float32, low / len(pieces), top_value / len(pieces))
        loudness = loudness * jnp.repeat(jnp.exp(draws), extent[dim] // shards_of).reshape((-1,) + (1,) * (len(extent) - 1 - dim))
    return loudness


def centred(own_key, dims, scale, bound, pieces=(), kind=jnp.bfloat16):
    loudness = level_of(own_key, dims, pieces, -0.22, 0.18) if pieces else 1.0
    drawn = jax.random.normal(own_key, dims, jnp.float32) * scale * loudness
    return jnp.minimum(jnp.maximum(drawn, -bound), bound).astype(kind)


def setup_inputs(seed: int = 0) -> dict:
    splits = jax.random.split(jax.random.key(seed), 6)
    slice_ops = centred(splits[0], (SLICES, S, S), 1.0, 6.0, ((0, 64), (1, 2)))
    base_op = centred(splits[1], (S, S), 1.0, 6.0)
    load_table = jnp.clip(jax.random.uniform(splits[2], (PHASES, S), jnp.float32, -1.0, 1.0), -1.0, 1.0)
    phase_idx = plant(jax.random.randint(splits[3], (SLICES, SUB), 0, PHASES), jax.random.fold_in(splits[3], 1), 0, PHASES - 1).astype(jnp.int32)
    step_counts = plant(jax.random.randint(splits[4], (SLICES, SUB), 1, 9), jax.random.fold_in(splits[4], 1), 1, 8).astype(jnp.int32)
    return {"slice_ops": slice_ops, "base_op": base_op, "load_table": load_table, "phase_idx": phase_idx, "step_counts": step_counts}


def reference(slice_ops, base_op, load_table, phase_idx, step_counts):
    norm_scale = 1.0 / math.sqrt(S)

    def slice_transfer(operands):
        slice_op, index_row, count_row = operands
        gain_rows = jnp.exp(0.1 * count_row.astype(jnp.float32)[:, None] * load_table[index_row])
        right_factor = (base_op * gain_rows[0]).astype(jnp.bfloat16)
        left_factor = (slice_op * gain_rows[1]).astype(jnp.bfloat16)
        product = jnp.dot(left_factor, right_factor, preferred_element_type=jnp.float32)
        return (product * norm_scale).astype(jnp.bfloat16)
    current = lax.map(slice_transfer, (slice_ops, phase_idx, step_counts))

    def combine_pair(operands):
        later, earlier = operands
        product = jnp.dot(later, earlier, preferred_element_type=jnp.float32)
        return (product * norm_scale).astype(jnp.bfloat16)
    for depth_level in range(LEVELS):
        distance = 2 ** depth_level
        earlier_all = jnp.roll(current, distance, axis=0)
        current = lax.map(combine_pair, (current, earlier_all))
    return current
```

```python
import math

import jax
import jax.numpy as jnp
from jax import lax
from jax.sharding import PartitionSpec as P

LEVELS = 2


def moved(value, distance, row_offset):
    tm_count = lax.axis_size("tm")
    row_count = lax.axis_size("row")
    pairs = []
    for t in range(tm_count):
        for r in range(row_count):
            source = t * row_count + r
            target = ((t + distance) % tm_count) * row_count + (r + row_offset) % row_count
            pairs.append((source, target))
    return lax.ppermute(value, ("tm", "row"), pairs)


def shards(slice_ops, base_op, load_table, phase_idx, step_counts):
    state_size = base_op.shape[0]
    norm_scale = 1.0 / math.sqrt(state_size)
    phase_count = load_table.shape[0]
    row_count = lax.axis_size("row")
    half = slice_ops.shape[1]
    row = lax.axis_index("row")
    index_row = phase_idx[0]
    count_row = step_counts[0].astype(jnp.float32)
    one_hot = (
        index_row[:, None] == lax.broadcasted_iota(jnp.int32, (index_row.shape[0], phase_count), 1)
    ).astype(jnp.float32)
    table_rows = jnp.dot(one_hot, load_table, precision=lax.Precision.HIGHEST)
    gain_rows = jnp.exp(0.1 * count_row[:, None] * table_rows)
    right_factor = (base_op * gain_rows[0]).astype(jnp.bfloat16)
    left_factor = (slice_ops[0] * gain_rows[1]).astype(jnp.bfloat16)
    product = jnp.dot(left_factor, right_factor, preferred_element_type=jnp.float32)
    current = (product * norm_scale).astype(jnp.bfloat16)
    for depth_level in range(LEVELS):
        distance = 2**depth_level
        total = None
        for offset in range(row_count):
            earlier_rows = moved(current, distance, offset)
            source_row = (row - offset) % row_count
            columns = lax.dynamic_slice_in_dim(current, source_row * half, half, axis=1)
            part = jnp.dot(columns, earlier_rows, preferred_element_type=jnp.float32)
            total = part if total is None else total + part
        current = (total * norm_scale).astype(jnp.bfloat16)
    return current[None]


def solution(mesh):
    return jax.shard_map(
        shards,
        mesh=mesh,
        in_specs=(P("tm", "row", None), P(), P(), P("tm", None), P("tm", None)),
        out_specs=P("tm", "row", None),
        check_vma=False,
    )
```

```python
import math

import jax
import jax.numpy as jnp
from jax import lax
from jax.sharding import PartitionSpec as P

LEVELS = 2
CHUNKS = 4


def sent(value, route):
    tm_count = lax.axis_size("tm")
    row_count = lax.axis_size("row")
    pairs = []
    for t in range(tm_count):
        for r in range(row_count):
            target = route(t, r, tm_count, row_count)
            if target is not None:
                pairs.append((t * row_count + r, target[0] * row_count + target[1]))
    return lax.ppermute(value, ("tm", "row"), pairs)


def y_low(t):
    return (t // 2) % 2


def direct(distance, row_offset):
    return lambda t, r, n, m: ((t + distance) % n, (r + row_offset) % m)


def when_low(low, route):
    return lambda t, r, n, m: route(t, r, n, m) if y_low(t) == low else None


def shards(slice_ops, base_op, load_table, phase_idx, step_counts):
    state_size = base_op.shape[0]
    norm_scale = 1.0 / math.sqrt(state_size)
    phase_count = load_table.shape[0]
    row_count = lax.axis_size("row")
    half = slice_ops.shape[1]
    row = lax.axis_index("row")
    index_row = phase_idx[0]
    count_row = step_counts[0].astype(jnp.float32)
    one_hot = (
        index_row[:, None] == lax.broadcasted_iota(jnp.int32, (index_row.shape[0], phase_count), 1)
    ).astype(jnp.float32)
    table_rows = jnp.dot(one_hot, load_table, precision=lax.Precision.HIGHEST)
    gain_rows = jnp.exp(0.1 * count_row[:, None] * table_rows)
    right_factor = (base_op * gain_rows[0]).astype(jnp.bfloat16)
    left_factor = (slice_ops[0] * gain_rows[1]).astype(jnp.bfloat16)
    product = jnp.dot(left_factor, right_factor, preferred_element_type=jnp.float32)
    current = (product * norm_scale).astype(jnp.bfloat16)

    total = None
    for offset in range(row_count):
        earlier_rows = sent(current, direct(1, offset))
        source_row = (row - offset) % row_count
        columns = lax.dynamic_slice_in_dim(current, source_row * half, half, axis=1)
        part = jnp.dot(columns, earlier_rows, preferred_element_type=jnp.float32)
        total = part if total is None else total + part
    current = (total * norm_scale).astype(jnp.bfloat16)

    own_columns = lax.dynamic_slice_in_dim(current, row * half, half, axis=1)
    other_columns = lax.dynamic_slice_in_dim(current, (1 - row) * half, half, axis=1)
    rows_each = half // CHUNKS
    total = None
    for chunk in range(CHUNKS):
        block = current[chunk * rows_each:(chunk + 1) * rows_each]
        same_near = sent(block, when_low(0, direct(2, 0)))
        other_near = sent(block, when_low(0, direct(2, 1)))
        ring_first = sent(block, when_low(1, direct(4, 0)))
        same_far = sent(ring_first, when_low(1, direct(-2, 0)))
        y_first = sent(block, when_low(1, direct(-2, 1)))
        other_far = sent(y_first, when_low(0, direct(4, 0)))
        same = same_near + same_far
        other = other_near + other_far
        span = slice(chunk * rows_each, (chunk + 1) * rows_each)
        part = jnp.dot(own_columns[:, span], same, preferred_element_type=jnp.float32)
        part = part + jnp.dot(other_columns[:, span], other, preferred_element_type=jnp.float32)
        total = part if total is None else total + part
    current = (total * norm_scale).astype(jnp.bfloat16)
    return current[None]


def solution(mesh):
    return jax.shard_map(
        shards,
        mesh=mesh,
        in_specs=(P("tm", "row", None), P(), P(), P("tm", None), P("tm", None)),
        out_specs=P("tm", "row", None),
        check_vma=False,
    )
```

```python
import math

import jax
import jax.numpy as jnp
from jax import lax
from jax.sharding import PartitionSpec as P

LEVELS = 2
DIRECT_ROWS = 352


def sent(value, route):
    tm_count = lax.axis_size("tm")
    row_count = lax.axis_size("row")
    pairs = []
    for t in range(tm_count):
        for r in range(row_count):
            target = route(t, r, tm_count, row_count)
            if target is not None:
                pairs.append((t * row_count + r, target[0] * row_count + target[1]))
    return lax.ppermute(value, ("tm", "row"), pairs)


def y_low(t):
    return (t // 2) % 2


def direct(distance, row_offset):
    return lambda t, r, n, m: ((t + distance) % n, (r + row_offset) % m)


def when_low(low, route):
    return lambda t, r, n, m: route(t, r, n, m) if y_low(t) == low else None


def shards(slice_ops, base_op, load_table, phase_idx, step_counts):
    state_size = base_op.shape[0]
    norm_scale = 1.0 / math.sqrt(state_size)
    phase_count = load_table.shape[0]
    row_count = lax.axis_size("row")
    half = slice_ops.shape[1]
    row = lax.axis_index("row")
    index_row = phase_idx[0]
    count_row = step_counts[0].astype(jnp.float32)
    one_hot = (
        index_row[:, None] == lax.broadcasted_iota(jnp.int32, (index_row.shape[0], phase_count), 1)
    ).astype(jnp.float32)
    table_rows = jnp.dot(one_hot, load_table, precision=lax.Precision.HIGHEST)
    gain_rows = jnp.exp(0.1 * count_row[:, None] * table_rows)
    right_factor = (base_op * gain_rows[0]).astype(jnp.bfloat16)
    left_factor = (slice_ops[0] * gain_rows[1]).astype(jnp.bfloat16)
    product = jnp.dot(left_factor, right_factor, preferred_element_type=jnp.float32)
    current = (product * norm_scale).astype(jnp.bfloat16)

    total = None
    for offset in range(row_count):
        earlier_rows = sent(current, direct(1, offset))
        source_row = (row - offset) % row_count
        columns = lax.dynamic_slice_in_dim(current, source_row * half, half, axis=1)
        part = jnp.dot(columns, earlier_rows, preferred_element_type=jnp.float32)
        total = part if total is None else total + part
    current = (total * norm_scale).astype(jnp.bfloat16)

    direct_rows = DIRECT_ROWS
    same = sent(current, direct(2, 0))
    other_near = sent(current, when_low(0, direct(2, 1)))
    other_top = sent(current[:direct_rows], when_low(1, direct(2, 1)))
    ring_first = sent(current[direct_rows:], when_low(1, direct(4, 0)))
    other_bottom = sent(ring_first, when_low(1, direct(-2, 1)))
    other_top = other_top + other_near[:direct_rows]
    other_bottom = other_bottom + other_near[direct_rows:]
    own_columns = lax.dynamic_slice_in_dim(current, row * half, half, axis=1)
    other_columns = lax.dynamic_slice_in_dim(current, (1 - row) * half, half, axis=1)
    total = jnp.dot(own_columns, same, preferred_element_type=jnp.float32)
    total = total + jnp.dot(other_columns[:, :direct_rows], other_top, preferred_element_type=jnp.float32)
    total = total + jnp.dot(other_columns[:, direct_rows:], other_bottom, preferred_element_type=jnp.float32)
    current = (total * norm_scale).astype(jnp.bfloat16)
    return current[None]


def solution(mesh):
    return jax.shard_map(
        shards,
        mesh=mesh,
        in_specs=(P("tm", "row", None), P(), P(), P("tm", None), P("tm", None)),
        out_specs=P("tm", "row", None),
        check_vma=False,
    )
```

```python
import math

import jax
import jax.numpy as jnp
from jax import lax
from jax.sharding import PartitionSpec as P

LEVELS = 2
DIRECT_ROWS = 352


def sent(value, route):
    tm_count = lax.axis_size("tm")
    row_count = lax.axis_size("row")
    pairs = []
    for t in range(tm_count):
        for r in range(row_count):
            target = route(t, r, tm_count, row_count)
            if target is not None:
                pairs.append((t * row_count + r, target[0] * row_count + target[1]))
    return lax.ppermute(value, ("tm", "row"), pairs)


def y_low(t):
    return (t // 2) % 2


def direct(distance, row_offset):
    return lambda t, r, n, m: ((t + distance) % n, (r + row_offset) % m)


def ring_of(t):
    return (t // 4) % 4


def ring_first_hop(t, r, n, m):
    if y_low(t) != 1:
        return None
    if ring_of(t) == 3:
        return ((t - 12) % n, r)
    return ((t + 4) % n, r)


def ring_first_exit(t, r, n, m):
    if y_low(t) != 1:
        return None
    if ring_of(t) == 0:
        return ((t + 14) % n, 1 - r)
    return ((t - 2) % n, 1 - r)


def when_low(low, route):
    return lambda t, r, n, m: route(t, r, n, m) if y_low(t) == low else None


def shards(slice_ops, base_op, load_table, phase_idx, step_counts):
    state_size = base_op.shape[0]
    norm_scale = 1.0 / math.sqrt(state_size)
    phase_count = load_table.shape[0]
    row_count = lax.axis_size("row")
    half = slice_ops.shape[1]
    row = lax.axis_index("row")
    index_row = phase_idx[0]
    count_row = step_counts[0].astype(jnp.float32)
    one_hot = (
        index_row[:, None] == lax.broadcasted_iota(jnp.int32, (index_row.shape[0], phase_count), 1)
    ).astype(jnp.float32)
    table_rows = jnp.dot(one_hot, load_table, precision=lax.Precision.HIGHEST)
    gain_rows = jnp.exp(0.1 * count_row[:, None] * table_rows)
    right_factor = (base_op * gain_rows[0]).astype(jnp.bfloat16)
    left_factor = (slice_ops[0] * gain_rows[1]).astype(jnp.bfloat16)
    product = jnp.dot(left_factor, right_factor, preferred_element_type=jnp.float32)
    current = (product * norm_scale).astype(jnp.bfloat16)

    total = None
    for offset in range(row_count):
        earlier_rows = sent(current, direct(1, offset))
        source_row = (row - offset) % row_count
        columns = lax.dynamic_slice_in_dim(current, source_row * half, half, axis=1)
        part = jnp.dot(columns, earlier_rows, preferred_element_type=jnp.float32)
        total = part if total is None else total + part
    current = (total * norm_scale).astype(jnp.bfloat16)

    direct_rows = DIRECT_ROWS
    same = sent(current, direct(2, 0))
    other_near = sent(current, when_low(0, direct(2, 1)))
    other_top = sent(current[:direct_rows], when_low(1, direct(2, 1)))
    ring_first = sent(current[direct_rows:], ring_first_hop)
    other_bottom = sent(ring_first, ring_first_exit)
    other_top = other_top + other_near[:direct_rows]
    other_bottom = other_bottom + other_near[direct_rows:]
    own_columns = lax.dynamic_slice_in_dim(current, row * half, half, axis=1)
    other_columns = lax.dynamic_slice_in_dim(current, (1 - row) * half, half, axis=1)
    total = jnp.dot(own_columns, same, preferred_element_type=jnp.float32)
    total = total + jnp.dot(other_columns[:, :direct_rows], other_top, preferred_element_type=jnp.float32)
    total = total + jnp.dot(other_columns[:, direct_rows:], other_bottom, preferred_element_type=jnp.float32)
    current = (total * norm_scale).astype(jnp.bfloat16)
    return current[None]


def solution(mesh):
    return jax.shard_map(
        shards,
        mesh=mesh,
        in_specs=(P("tm", "row", None), P(), P(), P("tm", None), P("tm", None)),
        out_specs=P("tm", "row", None),
        check_vma=False,
    )
```

```python
import math

import jax
import jax.numpy as jnp
from jax import lax
from jax.sharding import PartitionSpec as P

LEVELS = 2
DIRECT_ROWS = 352


def sent(value, route):
    tm_count = lax.axis_size("tm")
    row_count = lax.axis_size("row")
    pairs = []
    for t in range(tm_count):
        for r in range(row_count):
            target = route(t, r, tm_count, row_count)
            if target is not None:
                pairs.append((t * row_count + r, target[0] * row_count + target[1]))
    return lax.ppermute(value, ("tm", "row"), pairs)


def y_low(t):
    return (t // 2) % 2


def direct(distance, row_offset):
    return lambda t, r, n, m: ((t + distance) % n, (r + row_offset) % m)


def ring_of(t):
    return (t // 4) % 4


def ring_first_hop(t, r, n, m):
    if y_low(t) != 1:
        return None
    if ring_of(t) == 3:
        return ((t - 12) % n, r)
    return ((t + 4) % n, r)


def ring_first_exit(t, r, n, m):
    if y_low(t) != 1:
        return None
    if ring_of(t) == 0:
        return ((t + 14) % n, 1 - r)
    return ((t - 2) % n, 1 - r)


def when_low(low, route):
    return lambda t, r, n, m: route(t, r, n, m) if y_low(t) == low else None


def shards(slice_ops, base_op, load_table, phase_idx, step_counts):
    state_size = base_op.shape[0]
    norm_scale = 1.0 / math.sqrt(state_size)
    phase_count = load_table.shape[0]
    row_count = lax.axis_size("row")
    half = slice_ops.shape[1]
    row = lax.axis_index("row")
    index_row = phase_idx[0]
    count_row = step_counts[0].astype(jnp.float32)
    one_hot = (
        index_row[:, None] == lax.broadcasted_iota(jnp.int32, (index_row.shape[0], phase_count), 1)
    ).astype(jnp.float32)
    table_rows = jnp.dot(one_hot, load_table, precision=lax.Precision.HIGHEST)
    gain_rows = jnp.exp(0.1 * count_row[:, None] * table_rows)
    right_factor = (base_op * gain_rows[0]).astype(jnp.bfloat16)
    left_factor = (slice_ops[0] * gain_rows[1]).astype(jnp.bfloat16)
    product = jnp.dot(left_factor, right_factor, preferred_element_type=jnp.float32)
    current = (product * norm_scale).astype(jnp.bfloat16)

    split_rows = half // 2
    boundary = lambda t, r, n, m: ((t - 12) % n, r) if ring_of(t) == 3 and t % 4 == 3 else None
    boundary_exit = lambda t, r, n, m: ((t + 13) % n, r) if ring_of(t) == 0 and t % 4 == 3 else None
    not_boundary = lambda t, r, n, m: None if ring_of(t) == 3 and t % 4 == 3 else ((t + 1) % n, r)
    same_top = sent(current[:split_rows], direct(1, 0))
    same_bottom = sent(current[split_rows:], not_boundary)
    wrapped = sent(current[split_rows:], boundary)
    same_bottom = same_bottom + sent(wrapped, boundary_exit)
    other = sent(current, direct(1, 1))
    own_columns = lax.dynamic_slice_in_dim(current, row * half, half, axis=1)
    other_columns = lax.dynamic_slice_in_dim(current, (1 - row) * half, half, axis=1)
    total = jnp.dot(other_columns, other, preferred_element_type=jnp.float32)
    total = total + jnp.dot(own_columns[:, :split_rows], same_top, preferred_element_type=jnp.float32)
    total = total + jnp.dot(own_columns[:, split_rows:], same_bottom, preferred_element_type=jnp.float32)
    current = (total * norm_scale).astype(jnp.bfloat16)

    direct_rows = DIRECT_ROWS
    same = sent(current, direct(2, 0))
    other_near = sent(current, when_low(0, direct(2, 1)))
    other_top = sent(current[:direct_rows], when_low(1, direct(2, 1)))
    ring_first = sent(current[direct_rows:], ring_first_hop)
    other_bottom = sent(ring_first, ring_first_exit)
    other_top = other_top + other_near[:direct_rows]
    other_bottom = other_bottom + other_near[direct_rows:]
    own_columns = lax.dynamic_slice_in_dim(current, row * half, half, axis=1)
    other_columns = lax.dynamic_slice_in_dim(current, (1 - row) * half, half, axis=1)
    total = jnp.dot(own_columns, same, preferred_element_type=jnp.float32)
    total = total + jnp.dot(other_columns[:, :direct_rows], other_top, preferred_element_type=jnp.float32)
    total = total + jnp.dot(other_columns[:, direct_rows:], other_bottom, preferred_element_type=jnp.float32)
    current = (total * norm_scale).astype(jnp.bfloat16)
    return current[None]


def solution(mesh):
    return jax.shard_map(
        shards,
        mesh=mesh,
        in_specs=(P("tm", "row", None), P(), P(), P("tm", None), P("tm", None)),
        out_specs=P("tm", "row", None),
        check_vma=False,
    )
```

```python
import math

import jax
import jax.numpy as jnp
from jax import lax
from jax.sharding import PartitionSpec as P

LEVELS = 2
DIRECT_ROWS = 352


def sent(value, route):
    tm_count = lax.axis_size("tm")
    row_count = lax.axis_size("row")
    pairs = []
    for t in range(tm_count):
        for r in range(row_count):
            target = route(t, r, tm_count, row_count)
            if target is not None:
                pairs.append((t * row_count + r, target[0] * row_count + target[1]))
    return lax.ppermute(value, ("tm", "row"), pairs)


def y_low(t):
    return (t // 2) % 2


def direct(distance, row_offset):
    return lambda t, r, n, m: ((t + distance) % n, (r + row_offset) % m)


def ring_of(t):
    return (t // 4) % 4


def ring_first_hop(t, r, n, m):
    if y_low(t) != 1:
        return None
    if ring_of(t) == 3:
        return ((t - 12) % n, r)
    return ((t + 4) % n, r)


def ring_first_exit(t, r, n, m):
    if y_low(t) != 1:
        return None
    if ring_of(t) == 0:
        return ((t + 14) % n, 1 - r)
    return ((t - 2) % n, 1 - r)


def when_low(low, route):
    return lambda t, r, n, m: route(t, r, n, m) if y_low(t) == low else None


def combined(later, earlier, row, half, norm_scale):
    own_columns = lax.dynamic_slice_in_dim(later, row * half, half, axis=1)
    other_columns = lax.dynamic_slice_in_dim(later, (1 - row) * half, half, axis=1)
    columns = jnp.concatenate([own_columns, other_columns], axis=1)
    total = jnp.dot(columns, earlier, preferred_element_type=jnp.float32)
    return (total * norm_scale).astype(jnp.bfloat16)


def shards(slice_ops, base_op, load_table, phase_idx, step_counts):
    state_size = base_op.shape[0]
    norm_scale = 1.0 / math.sqrt(state_size)
    phase_count = load_table.shape[0]
    row_count = lax.axis_size("row")
    half = slice_ops.shape[1]
    row = lax.axis_index("row")
    index_row = phase_idx[0]
    count_row = step_counts[0].astype(jnp.float32)
    one_hot = (
        index_row[:, None] == lax.broadcasted_iota(jnp.int32, (index_row.shape[0], phase_count), 1)
    ).astype(jnp.float32)
    table_rows = jnp.dot(one_hot, load_table, precision=lax.Precision.HIGHEST)
    gain_rows = jnp.exp(0.1 * count_row[:, None] * table_rows)
    right_factor = (base_op * gain_rows[0]).astype(jnp.bfloat16)
    left_factor = (slice_ops[0] * gain_rows[1]).astype(jnp.bfloat16)
    product = jnp.dot(left_factor, right_factor, preferred_element_type=jnp.float32)
    current = (product * norm_scale).astype(jnp.bfloat16)

    split_rows = half // 2
    boundary = lambda t, r, n, m: ((t - 12) % n, r) if ring_of(t) == 3 and t % 4 == 3 else None
    boundary_exit = lambda t, r, n, m: ((t + 13) % n, r) if ring_of(t) == 0 and t % 4 == 3 else None
    not_boundary = lambda t, r, n, m: None if ring_of(t) == 3 and t % 4 == 3 else ((t + 1) % n, r)
    same_top = sent(current[:split_rows], direct(1, 0))
    same_bottom = sent(current[split_rows:], not_boundary)
    wrapped = sent(current[split_rows:], boundary)
    same_bottom = same_bottom + sent(wrapped, boundary_exit)
    other = sent(current, direct(1, 1))
    earlier = jnp.concatenate([same_top, same_bottom, other], axis=0)
    current = combined(current, earlier, row, half, norm_scale)

    direct_rows = DIRECT_ROWS
    same = sent(current, direct(2, 0))
    other_near = sent(current, when_low(0, direct(2, 1)))
    other_top = sent(current[:direct_rows], when_low(1, direct(2, 1)))
    ring_first = sent(current[direct_rows:], ring_first_hop)
    other_bottom = sent(ring_first, ring_first_exit)
    other_top = other_top + other_near[:direct_rows]
    other_bottom = other_bottom + other_near[direct_rows:]
    earlier = jnp.concatenate([same, other_top, other_bottom], axis=0)
    current = combined(current, earlier, row, half, norm_scale)
    return current[None]


def solution(mesh):
    return jax.shard_map(
        shards,
        mesh=mesh,
        in_specs=(P("tm", "row", None), P(), P(), P("tm", None), P("tm", None)),
        out_specs=P("tm", "row", None),
        check_vma=False,
    )
```

```python
import math

import jax
import jax.numpy as jnp
from jax import lax
from jax.sharding import PartitionSpec as P

LEVELS = 2
DIRECT_ROWS = 208
RELAY_ROWS = (416, 400)


def sent(value, route):
    tm_count = lax.axis_size("tm")
    row_count = lax.axis_size("row")
    pairs = []
    for t in range(tm_count):
        for r in range(row_count):
            target = route(t, r, tm_count, row_count)
            if target is not None:
                pairs.append((t * row_count + r, target[0] * row_count + target[1]))
    return lax.ppermute(value, ("tm", "row"), pairs)


def y_low(t):
    return (t // 2) % 2


def direct(distance, row_offset):
    return lambda t, r, n, m: ((t + distance) % n, (r + row_offset) % m)


def ring_of(t):
    return (t // 4) % 4


def ring_first_hop(t, r, n, m):
    if y_low(t) != 1:
        return None
    if ring_of(t) == 3:
        return ((t - 12) % n, r)
    return ((t + 4) % n, r)


def ring_first_exit(t, r, n, m):
    if y_low(t) != 1:
        return None
    if ring_of(t) == 0:
        return ((t + 14) % n, 1 - r)
    return ((t - 2) % n, 1 - r)


def when_low(low, route):
    return lambda t, r, n, m: route(t, r, n, m) if y_low(t) == low else None


def combined(later, own_rows, other_rows, row, norm_scale):
    earlier = jnp.where(
        row == 0,
        jnp.concatenate(own_rows + other_rows, axis=0),
        jnp.concatenate(other_rows + own_rows, axis=0),
    )
    total = jnp.dot(later, earlier, preferred_element_type=jnp.float32)
    return (total * norm_scale).astype(jnp.bfloat16)


def shards(slice_ops, base_op, load_table, phase_idx, step_counts):
    state_size = base_op.shape[0]
    norm_scale = 1.0 / math.sqrt(state_size)
    phase_count = load_table.shape[0]
    row_count = lax.axis_size("row")
    half = slice_ops.shape[1]
    row = lax.axis_index("row")
    index_row = phase_idx[0]
    count_row = step_counts[0].astype(jnp.float32)
    one_hot = (
        index_row[:, None] == lax.broadcasted_iota(jnp.int32, (index_row.shape[0], phase_count), 1)
    ).astype(jnp.float32)
    table_rows = jnp.dot(one_hot, load_table, precision=lax.Precision.HIGHEST)
    gain_rows = jnp.exp(0.1 * count_row[:, None] * table_rows)
    right_factor = (base_op * gain_rows[0]).astype(jnp.bfloat16)
    left_factor = (slice_ops[0] * gain_rows[1]).astype(jnp.bfloat16)
    product = jnp.dot(left_factor, right_factor, preferred_element_type=jnp.float32)
    current = (product * norm_scale).astype(jnp.bfloat16)

    split_rows = half // 2
    boundary = lambda t, r, n, m: ((t - 12) % n, r) if ring_of(t) == 3 and t % 4 == 3 else None
    boundary_exit = lambda t, r, n, m: ((t + 13) % n, r) if ring_of(t) == 0 and t % 4 == 3 else None
    not_boundary = lambda t, r, n, m: None if ring_of(t) == 3 and t % 4 == 3 else ((t + 1) % n, r)
    same_top = sent(current[:split_rows], direct(1, 0))
    same_bottom = sent(current[split_rows:], not_boundary)
    wrapped = sent(current[split_rows:], boundary)
    same_bottom = same_bottom + sent(wrapped, boundary_exit)
    other = sent(current, direct(1, 1))
    current = combined(current, [same_top, same_bottom], [other], row, norm_scale)

    same = sent(current, direct(2, 0))
    other_near = sent(current, when_low(0, direct(2, 1)))
    other_rows = [sent(current[:DIRECT_ROWS], when_low(1, direct(2, 1))) + other_near[:DIRECT_ROWS]]
    begin = DIRECT_ROWS
    for size in RELAY_ROWS:
        ring_first = sent(current[begin:begin + size], ring_first_hop)
        other_rows.append(sent(ring_first, ring_first_exit) + other_near[begin:begin + size])
        begin += size
    current = combined(current, [same], other_rows, row, norm_scale)
    return current[None]


def solution(mesh):
    return jax.shard_map(
        shards,
        mesh=mesh,
        in_specs=(P("tm", "row", None), P(), P(), P("tm", None), P("tm", None)),
        out_specs=P("tm", "row", None),
        check_vma=False,
    )
```

```python
import math

import jax
import jax.numpy as jnp
from jax import lax
from jax.sharding import PartitionSpec as P

LEVELS = 2
DIRECT_ROWS = 96


def sent(value, route):
    tm_count = lax.axis_size("tm")
    row_count = lax.axis_size("row")
    pairs = []
    for t in range(tm_count):
        for r in range(row_count):
            target = route(t, r, tm_count, row_count)
            if target is not None:
                pairs.append((t * row_count + r, target[0] * row_count + target[1]))
    return lax.ppermute(value, ("tm", "row"), pairs)


def y_low(t):
    return (t // 2) % 2


def direct(distance, row_offset):
    return lambda t, r, n, m: ((t + distance) % n, (r + row_offset) % m)


def ring_of(t):
    return (t // 4) % 4


def ring_first_hop(t, r, n, m):
    if y_low(t) != 1:
        return None
    if ring_of(t) == 3:
        return ((t - 12) % n, r)
    return ((t + 4) % n, r)


def ring_first_exit(t, r, n, m):
    if y_low(t) != 1:
        return None
    if ring_of(t) == 0:
        return ((t + 14) % n, 1 - r)
    return ((t - 2) % n, 1 - r)


def when_low(low, route):
    return lambda t, r, n, m: route(t, r, n, m) if y_low(t) == low else None


def natural(own_rows, other_rows, row):
    return jnp.where(
        row == 0,
        jnp.concatenate(own_rows + other_rows, axis=0),
        jnp.concatenate(other_rows + own_rows, axis=0),
    )


def level_product(later, earlier, norm_scale):
    total = jnp.dot(later, earlier, preferred_element_type=jnp.float32)
    return (total * norm_scale).astype(jnp.bfloat16)


def shards(slice_ops, base_op, load_table, phase_idx, step_counts):
    state_size = base_op.shape[0]
    norm_scale = 1.0 / math.sqrt(state_size)
    phase_count = load_table.shape[0]
    row_count = lax.axis_size("row")
    half = slice_ops.shape[1]
    row = lax.axis_index("row")
    index_row = phase_idx[0]
    count_row = step_counts[0].astype(jnp.float32)
    one_hot = (
        index_row[:, None] == lax.broadcasted_iota(jnp.int32, (index_row.shape[0], phase_count), 1)
    ).astype(jnp.float32)
    table_rows = jnp.dot(one_hot, load_table, precision=lax.Precision.HIGHEST)
    gain_rows = jnp.exp(0.1 * count_row[:, None] * table_rows)
    right_factor = (base_op * gain_rows[0]).astype(jnp.bfloat16)
    left_factor = (slice_ops[0] * gain_rows[1]).astype(jnp.bfloat16)
    chunk_rows = half // 2
    chunks = []
    for c in range(2):
        product = jnp.dot(left_factor[c * chunk_rows:(c + 1) * chunk_rows], right_factor,
                          preferred_element_type=jnp.float32)
        chunks.append((product * norm_scale).astype(jnp.bfloat16))

    boundary = lambda t, r, n, m: ((t - 12) % n, r) if ring_of(t) == 3 and t % 4 == 3 else None
    boundary_exit = lambda t, r, n, m: ((t + 13) % n, r) if ring_of(t) == 0 and t % 4 == 3 else None
    not_boundary = lambda t, r, n, m: None if ring_of(t) == 3 and t % 4 == 3 else ((t + 1) % n, r)
    own_rows = [sent(chunks[0], direct(1, 0))]
    other_rows = [sent(chunks[0], direct(1, 1))]
    own_rows.append(sent(chunks[1], not_boundary) + sent(sent(chunks[1], boundary), boundary_exit))
    other_rows.append(sent(chunks[1], direct(1, 1)))
    earlier = natural(own_rows, other_rows, row)
    chunks = [level_product(chunk, earlier, norm_scale) for chunk in chunks]

    own_rows = []
    other_rows = []
    for chunk in chunks:
        own_rows.append(sent(chunk, direct(2, 0)))
        other_near = sent(chunk, when_low(0, direct(2, 1)))
        other_rows.append(sent(chunk[:DIRECT_ROWS], when_low(1, direct(2, 1))) + other_near[:DIRECT_ROWS])
        ring_first = sent(chunk[DIRECT_ROWS:], ring_first_hop)
        other_rows.append(sent(ring_first, ring_first_exit) + other_near[DIRECT_ROWS:])
    earlier = natural(own_rows, other_rows, row)
    current = level_product(jnp.concatenate(chunks, axis=0), earlier, norm_scale)
    return current[None]


def solution(mesh):
    return jax.shard_map(
        shards,
        mesh=mesh,
        in_specs=(P("tm", "row", None), P(), P(), P("tm", None), P("tm", None)),
        out_specs=P("tm", "row", None),
        check_vma=False,
    )
```

```python
import math

import jax
import jax.numpy as jnp
from jax import lax
from jax.sharding import PartitionSpec as P

LEVELS = 2
DIRECT_ROWS = 208
RELAY_ROWS = (416, 400)


def sent(value, route):
    tm_count = lax.axis_size("tm")
    row_count = lax.axis_size("row")
    pairs = []
    for t in range(tm_count):
        for r in range(row_count):
            target = route(t, r, tm_count, row_count)
            if target is not None:
                pairs.append((t * row_count + r, target[0] * row_count + target[1]))
    return lax.ppermute(value, ("tm", "row"), pairs)


def y_low(t):
    return (t // 2) % 2


def direct(distance, row_offset):
    return lambda t, r, n, m: ((t + distance) % n, (r + row_offset) % m)


def ring_of(t):
    return (t // 4) % 4


def ring_first_hop(t, r, n, m):
    if y_low(t) != 1:
        return None
    if ring_of(t) == 3:
        return ((t - 12) % n, r)
    return ((t + 4) % n, r)


def ring_first_exit(t, r, n, m):
    if y_low(t) != 1:
        return None
    if ring_of(t) == 0:
        return ((t + 14) % n, 1 - r)
    return ((t - 2) % n, 1 - r)


def when_low(low, route):
    return lambda t, r, n, m: route(t, r, n, m) if y_low(t) == low else None


def natural(own_rows, other_rows, row):
    return jnp.where(
        row == 0,
        jnp.concatenate(own_rows + other_rows, axis=0),
        jnp.concatenate(other_rows + own_rows, axis=0),
    )


def level_product(later, earlier, norm_scale):
    total = jnp.dot(later, earlier, preferred_element_type=jnp.float32)
    return (total * norm_scale).astype(jnp.bfloat16)


def shards(slice_ops, base_op, load_table, phase_idx, step_counts):
    state_size = base_op.shape[0]
    norm_scale = 1.0 / math.sqrt(state_size)
    phase_count = load_table.shape[0]
    row_count = lax.axis_size("row")
    half = slice_ops.shape[1]
    row = lax.axis_index("row")
    index_row = phase_idx[0]
    count_row = step_counts[0].astype(jnp.float32)
    one_hot = (
        index_row[:, None] == lax.broadcasted_iota(jnp.int32, (index_row.shape[0], phase_count), 1)
    ).astype(jnp.float32)
    table_rows = jnp.dot(one_hot, load_table, precision=lax.Precision.HIGHEST)
    gain_rows = jnp.exp(0.1 * count_row[:, None] * table_rows)
    right_factor = (base_op * gain_rows[0]).astype(jnp.bfloat16)
    left_factor = (slice_ops[0] * gain_rows[1]).astype(jnp.bfloat16)
    chunk_rows = half // 2
    chunks = []
    for c in range(2):
        product = jnp.dot(left_factor[c * chunk_rows:(c + 1) * chunk_rows], right_factor,
                          preferred_element_type=jnp.float32)
        chunks.append((product * norm_scale).astype(jnp.bfloat16))

    boundary = lambda t, r, n, m: ((t - 12) % n, r) if ring_of(t) == 3 and t % 4 == 3 else None
    boundary_exit = lambda t, r, n, m: ((t + 13) % n, r) if ring_of(t) == 0 and t % 4 == 3 else None
    not_boundary = lambda t, r, n, m: None if ring_of(t) == 3 and t % 4 == 3 else ((t + 1) % n, r)
    own_rows = [sent(chunks[0], direct(1, 0))]
    other_rows = [sent(chunks[0], direct(1, 1))]
    own_rows.append(sent(chunks[1], not_boundary) + sent(sent(chunks[1], boundary), boundary_exit))
    other_rows.append(sent(chunks[1], direct(1, 1)))
    earlier = natural(own_rows, other_rows, row)
    current = level_product(jnp.concatenate(chunks, axis=0), earlier, norm_scale)

    same = sent(current, direct(2, 0))
    other_near = sent(current, when_low(0, direct(2, 1)))
    other_rows = [sent(current[:DIRECT_ROWS], when_low(1, direct(2, 1))) + other_near[:DIRECT_ROWS]]
    begin = DIRECT_ROWS
    for size in RELAY_ROWS:
        ring_first = sent(current[begin:begin + size], ring_first_hop)
        other_rows.append(sent(ring_first, ring_first_exit) + other_near[begin:begin + size])
        begin += size
    current = level_product(current, natural([same], other_rows, row), norm_scale)
    return current[None]


def solution(mesh):
    return jax.shard_map(
        shards,
        mesh=mesh,
        in_specs=(P("tm", "row", None), P(), P(), P("tm", None), P("tm", None)),
        out_specs=P("tm", "row", None),
        check_vma=False,
    )
```

```python
import math

import jax
import jax.numpy as jnp
from jax import lax
from jax.sharding import PartitionSpec as P

LEVELS = 2


def sent(value, route):
    tm_count = lax.axis_size("tm")
    row_count = lax.axis_size("row")
    pairs = []
    for t in range(tm_count):
        for r in range(row_count):
            target = route(t, r, tm_count, row_count)
            if target is not None:
                pairs.append((t * row_count + r, target[0] * row_count + target[1]))
    return lax.ppermute(value, ("tm", "row"), pairs)


def y_low(t):
    return (t // 2) % 2


def direct(distance, row_offset):
    return lambda t, r, n, m: ((t + distance) % n, (r + row_offset) % m)


def ring_of(t):
    return (t // 4) % 4


def ring_first_hop(t, r, n, m):
    if y_low(t) != 1:
        return None
    if ring_of(t) == 3:
        return ((t - 12) % n, r)
    return ((t + 4) % n, r)


def handed_on(row_offset):
    def route(t, r, n, m):
        if y_low(t) != 1:
            return None
        if ring_of(t) == 0:
            return ((t + 14) % n, (r + row_offset) % m)
        return ((t - 2) % n, (r + row_offset) % m)
    return route


def when_low(low, route):
    return lambda t, r, n, m: route(t, r, n, m) if y_low(t) == low else None


def natural(own_rows, other_rows, row):
    return jnp.where(
        row == 0,
        jnp.concatenate(own_rows + other_rows, axis=0),
        jnp.concatenate(other_rows + own_rows, axis=0),
    )


def level_product(later, earlier, norm_scale):
    total = jnp.dot(later, earlier, preferred_element_type=jnp.float32)
    return (total * norm_scale).astype(jnp.bfloat16)


def shards(slice_ops, base_op, load_table, phase_idx, step_counts):
    state_size = base_op.shape[0]
    norm_scale = 1.0 / math.sqrt(state_size)
    phase_count = load_table.shape[0]
    row_count = lax.axis_size("row")
    half = slice_ops.shape[1]
    row = lax.axis_index("row")
    index_row = phase_idx[0]
    count_row = step_counts[0].astype(jnp.float32)
    one_hot = (
        index_row[:, None] == lax.broadcasted_iota(jnp.int32, (index_row.shape[0], phase_count), 1)
    ).astype(jnp.float32)
    table_rows = jnp.dot(one_hot, load_table, precision=lax.Precision.HIGHEST)
    gain_rows = jnp.exp(0.1 * count_row[:, None] * table_rows)
    right_factor = (base_op * gain_rows[0]).astype(jnp.bfloat16)
    left_factor = (slice_ops[0] * gain_rows[1]).astype(jnp.bfloat16)
    chunk_rows = half // 2
    chunks = []
    for c in range(2):
        product = jnp.dot(left_factor[c * chunk_rows:(c + 1) * chunk_rows], right_factor,
                          preferred_element_type=jnp.float32)
        chunks.append((product * norm_scale).astype(jnp.bfloat16))

    boundary = lambda t, r, n, m: ((t - 12) % n, r) if ring_of(t) == 3 and t % 4 == 3 else None
    boundary_exit = lambda t, r, n, m: ((t + 13) % n, r) if ring_of(t) == 0 and t % 4 == 3 else None
    not_boundary = lambda t, r, n, m: None if ring_of(t) == 3 and t % 4 == 3 else ((t + 1) % n, r)
    own_rows = [sent(chunks[0], direct(1, 0))]
    other_rows = [sent(chunks[0], direct(1, 1))]
    own_rows.append(sent(chunks[1], not_boundary) + sent(sent(chunks[1], boundary), boundary_exit))
    other_rows.append(sent(chunks[1], direct(1, 1)))
    earlier = natural(own_rows, other_rows, row)
    chunks = [level_product(chunk, earlier, norm_scale) for chunk in chunks]

    straight, handed = chunks
    crossed = sent(handed, ring_first_hop)
    same_straight = sent(straight, direct(2, 0))
    other_straight = sent(straight, direct(2, 1))
    onward = jnp.where(lax.axis_index("tm") // 2 % 2 == 0, handed, crossed)
    same_handed = sent(onward, lambda t, r, n, m: direct(2, 0)(t, r, n, m) if y_low(t) == 0 else handed_on(0)(t, r, n, m))
    other_handed = sent(onward, lambda t, r, n, m: direct(2, 1)(t, r, n, m) if y_low(t) == 0 else handed_on(1)(t, r, n, m))
    earlier = natural([same_straight, same_handed], [other_straight, other_handed], row)
    current = level_product(jnp.concatenate(chunks, axis=0), earlier, norm_scale)
    return current[None]


def solution(mesh):
    return jax.shard_map(
        shards,
        mesh=mesh,
        in_specs=(P("tm", "row", None), P(), P(), P("tm", None), P("tm", None)),
        out_specs=P("tm", "row", None),
        check_vma=False,
    )
```

```python
import math

import jax
import jax.numpy as jnp
from jax import lax
from jax.sharding import PartitionSpec as P

LEVELS = 2
RELAY_ROWS = (512, 512)


def sent(value, route):
    tm_count = lax.axis_size("tm")
    row_count = lax.axis_size("row")
    pairs = []
    for t in range(tm_count):
        for r in range(row_count):
            target = route(t, r, tm_count, row_count)
            if target is not None:
                pairs.append((t * row_count + r, target[0] * row_count + target[1]))
    return lax.ppermute(value, ("tm", "row"), pairs)


def y_low(t):
    return (t // 2) % 2


def direct(distance, row_offset):
    return lambda t, r, n, m: ((t + distance) % n, (r + row_offset) % m)


def ring_of(t):
    return (t // 4) % 4


def ring_first_hop(t, r, n, m):
    if y_low(t) != 1:
        return None
    if ring_of(t) == 3:
        return ((t - 12) % n, r)
    return ((t + 4) % n, r)


def ring_first_exit(t, r, n, m):
    if y_low(t) != 1:
        return None
    if ring_of(t) == 0:
        return ((t + 14) % n, 1 - r)
    return ((t - 2) % n, 1 - r)


def when_low(low, route):
    return lambda t, r, n, m: route(t, r, n, m) if y_low(t) == low else None


def natural(own_rows, other_rows, row):
    return jnp.where(
        row == 0,
        jnp.concatenate(own_rows + other_rows, axis=0),
        jnp.concatenate(other_rows + own_rows, axis=0),
    )


def level_product(later, earlier, norm_scale):
    total = jnp.dot(later, earlier, preferred_element_type=jnp.float32)
    return (total * norm_scale).astype(jnp.bfloat16)


def shards(slice_ops, base_op, load_table, phase_idx, step_counts):
    state_size = base_op.shape[0]
    norm_scale = 1.0 / math.sqrt(state_size)
    phase_count = load_table.shape[0]
    row_count = lax.axis_size("row")
    half = slice_ops.shape[1]
    row = lax.axis_index("row")
    index_row = phase_idx[0]
    count_row = step_counts[0].astype(jnp.float32)
    one_hot = (
        index_row[:, None] == lax.broadcasted_iota(jnp.int32, (index_row.shape[0], phase_count), 1)
    ).astype(jnp.float32)
    table_rows = jnp.dot(one_hot, load_table, precision=lax.Precision.HIGHEST)
    gain_rows = jnp.exp(0.1 * count_row[:, None] * table_rows)
    right_factor = (base_op * gain_rows[0]).astype(jnp.bfloat16)
    left_factor = (slice_ops[0] * gain_rows[1]).astype(jnp.bfloat16)
    chunk_rows = half // 2
    chunks = []
    for c in range(2):
        product = jnp.dot(left_factor[c * chunk_rows:(c + 1) * chunk_rows], right_factor,
                          preferred_element_type=jnp.float32)
        chunks.append((product * norm_scale).astype(jnp.bfloat16))

    boundary = lambda t, r, n, m: ((t - 12) % n, r) if ring_of(t) == 3 and t % 4 == 3 else None
    boundary_exit = lambda t, r, n, m: ((t + 13) % n, r) if ring_of(t) == 0 and t % 4 == 3 else None
    not_boundary = lambda t, r, n, m: None if ring_of(t) == 3 and t % 4 == 3 else ((t + 1) % n, r)
    own_rows = [sent(chunks[0], direct(1, 0))]
    other_rows = [sent(chunks[0], direct(1, 1))]
    own_rows.append(sent(chunks[1], not_boundary) + sent(sent(chunks[1], boundary), boundary_exit))
    other_rows.append(sent(chunks[1], direct(1, 1)))
    earlier = natural(own_rows, other_rows, row)
    current = level_product(jnp.concatenate(chunks, axis=0), earlier, norm_scale)

    same = sent(current, direct(2, 0))
    other_near = sent(current, when_low(0, direct(2, 1)))
    other_rows = []
    begin = 0
    for size in RELAY_ROWS:
        ring_first = sent(current[begin:begin + size], ring_first_hop)
        other_rows.append(sent(ring_first, ring_first_exit) + other_near[begin:begin + size])
        begin += size
    current = level_product(current, natural([same], other_rows, row), norm_scale)
    return current[None]


def solution(mesh):
    return jax.shard_map(
        shards,
        mesh=mesh,
        in_specs=(P("tm", "row", None), P(), P(), P("tm", None), P("tm", None)),
        out_specs=P("tm", "row", None),
        check_vma=False,
    )
```

```python
import math

import jax
import jax.numpy as jnp
from jax import lax
from jax.sharding import PartitionSpec as P

LEVELS = 2
DIRECT_ROWS = 304
RELAY_ROWS = (368, 352)


def sent(value, route):
    tm_count = lax.axis_size("tm")
    row_count = lax.axis_size("row")
    pairs = []
    for t in range(tm_count):
        for r in range(row_count):
            target = route(t, r, tm_count, row_count)
            if target is not None:
                pairs.append((t * row_count + r, target[0] * row_count + target[1]))
    return lax.ppermute(value, ("tm", "row"), pairs)


def y_low(t):
    return (t // 2) % 2


def direct(distance, row_offset):
    return lambda t, r, n, m: ((t + distance) % n, (r + row_offset) % m)


def ring_of(t):
    return (t // 4) % 4


def ring_first_hop(t, r, n, m):
    if y_low(t) != 1:
        return None
    if ring_of(t) == 3:
        return ((t - 12) % n, r)
    return ((t + 4) % n, r)


def ring_first_exit(t, r, n, m):
    if y_low(t) != 1:
        return None
    if ring_of(t) == 0:
        return ((t + 14) % n, 1 - r)
    return ((t - 2) % n, 1 - r)


def when_low(low, route):
    return lambda t, r, n, m: route(t, r, n, m) if y_low(t) == low else None


def natural(own_rows, other_rows, row):
    return jnp.where(
        row == 0,
        jnp.concatenate(own_rows + other_rows, axis=0),
        jnp.concatenate(other_rows + own_rows, axis=0),
    )


def level_product(later, earlier, norm_scale):
    total = jnp.dot(later, earlier, preferred_element_type=jnp.float32)
    return (total * norm_scale).astype(jnp.bfloat16)


def shards(slice_ops, base_op, load_table, phase_idx, step_counts):
    state_size = base_op.shape[0]
    norm_scale = 1.0 / math.sqrt(state_size)
    phase_count = load_table.shape[0]
    row_count = lax.axis_size("row")
    half = slice_ops.shape[1]
    row = lax.axis_index("row")
    index_row = phase_idx[0]
    count_row = step_counts[0].astype(jnp.float32)
    one_hot = (
        index_row[:, None] == lax.broadcasted_iota(jnp.int32, (index_row.shape[0], phase_count), 1)
    ).astype(jnp.float32)
    table_rows = jnp.dot(one_hot, load_table, precision=lax.Precision.HIGHEST)
    gain_rows = jnp.exp(0.1 * count_row[:, None] * table_rows)
    right_factor = (base_op * gain_rows[0]).astype(jnp.bfloat16)
    left_factor = (slice_ops[0] * gain_rows[1]).astype(jnp.bfloat16)
    chunk_rows = half // 2
    chunks = []
    for c in range(2):
        product = jnp.dot(left_factor[c * chunk_rows:(c + 1) * chunk_rows], right_factor,
                          preferred_element_type=jnp.float32)
        chunks.append((product * norm_scale).astype(jnp.bfloat16))

    boundary = lambda t, r, n, m: ((t - 12) % n, r) if ring_of(t) == 3 and t % 4 == 3 else None
    boundary_exit = lambda t, r, n, m: ((t + 13) % n, r) if ring_of(t) == 0 and t % 4 == 3 else None
    not_boundary = lambda t, r, n, m: None if ring_of(t) == 3 and t % 4 == 3 else ((t + 1) % n, r)
    own_rows = [sent(chunks[0], direct(1, 0))]
    other_rows = [sent(chunks[0], direct(1, 1))]
    own_rows.append(sent(chunks[1], not_boundary) + sent(sent(chunks[1], boundary), boundary_exit))
    other_rows.append(sent(chunks[1], direct(1, 1)))
    earlier = natural(own_rows, other_rows, row)
    current = level_product(jnp.concatenate(chunks, axis=0), earlier, norm_scale)

    same = sent(current, direct(2, 0))
    other_near = sent(current, when_low(0, direct(2, 1)))
    other_rows = [sent(current[:DIRECT_ROWS], when_low(1, direct(2, 1))) + other_near[:DIRECT_ROWS]]
    begin = DIRECT_ROWS
    for size in RELAY_ROWS:
        ring_first = sent(current[begin:begin + size], ring_first_hop)
        other_rows.append(sent(ring_first, ring_first_exit) + other_near[begin:begin + size])
        begin += size
    current = level_product(current, natural([same], other_rows, row), norm_scale)
    return current[None]


def solution(mesh):
    return jax.shard_map(
        shards,
        mesh=mesh,
        in_specs=(P("tm", "row", None), P(), P(), P("tm", None), P("tm", None)),
        out_specs=P("tm", "row", None),
        check_vma=False,
    )
```

```python
import math

import jax
import jax.numpy as jnp
from jax import lax
from jax.sharding import PartitionSpec as P

LEVELS = 2
DIRECT_ROWS = 400
RELAY_ROWS = (320, 304)


def sent(value, route):
    tm_count = lax.axis_size("tm")
    row_count = lax.axis_size("row")
    pairs = []
    for t in range(tm_count):
        for r in range(row_count):
            target = route(t, r, tm_count, row_count)
            if target is not None:
                pairs.append((t * row_count + r, target[0] * row_count + target[1]))
    return lax.ppermute(value, ("tm", "row"), pairs)


def y_low(t):
    return (t // 2) % 2


def direct(distance, row_offset):
    return lambda t, r, n, m: ((t + distance) % n, (r + row_offset) % m)


def ring_of(t):
    return (t // 4) % 4


def ring_first_hop(t, r, n, m):
    if y_low(t) != 1:
        return None
    if ring_of(t) == 3:
        return ((t - 12) % n, r)
    return ((t + 4) % n, r)


def ring_first_exit(t, r, n, m):
    if y_low(t) != 1:
        return None
    if ring_of(t) == 0:
        return ((t + 14) % n, 1 - r)
    return ((t - 2) % n, 1 - r)


def when_low(low, route):
    return lambda t, r, n, m: route(t, r, n, m) if y_low(t) == low else None


def natural(own_rows, other_rows, row):
    return jnp.where(
        row == 0,
        jnp.concatenate(own_rows + other_rows, axis=0),
        jnp.concatenate(other_rows + own_rows, axis=0),
    )


def level_product(later, earlier, norm_scale):
    total = jnp.dot(later, earlier, preferred_element_type=jnp.float32)
    return (total * norm_scale).astype(jnp.bfloat16)


def shards(slice_ops, base_op, load_table, phase_idx, step_counts):
    state_size = base_op.shape[0]
    norm_scale = 1.0 / math.sqrt(state_size)
    phase_count = load_table.shape[0]
    row_count = lax.axis_size("row")
    half = slice_ops.shape[1]
    row = lax.axis_index("row")
    index_row = phase_idx[0]
    count_row = step_counts[0].astype(jnp.float32)
    one_hot = (
        index_row[:, None] == lax.broadcasted_iota(jnp.int32, (index_row.shape[0], phase_count), 1)
    ).astype(jnp.float32)
    table_rows = jnp.dot(one_hot, load_table, precision=lax.Precision.HIGHEST)
    gain_rows = jnp.exp(0.1 * count_row[:, None] * table_rows)
    right_factor = (base_op * gain_rows[0]).astype(jnp.bfloat16)
    left_factor = (slice_ops[0] * gain_rows[1]).astype(jnp.bfloat16)
    chunk_rows = half // 2
    chunks = []
    for c in range(2):
        product = jnp.dot(left_factor[c * chunk_rows:(c + 1) * chunk_rows], right_factor,
                          preferred_element_type=jnp.float32)
        chunks.append((product * norm_scale).astype(jnp.bfloat16))

    boundary = lambda t, r, n, m: ((t - 12) % n, r) if ring_of(t) == 3 and t % 4 == 3 else None
    boundary_exit = lambda t, r, n, m: ((t + 13) % n, r) if ring_of(t) == 0 and t % 4 == 3 else None
    not_boundary = lambda t, r, n, m: None if ring_of(t) == 3 and t % 4 == 3 else ((t + 1) % n, r)
    own_rows = [sent(chunks[0], direct(1, 0))]
    other_rows = [sent(chunks[0], direct(1, 1))]
    own_rows.append(sent(chunks[1], not_boundary) + sent(sent(chunks[1], boundary), boundary_exit))
    other_rows.append(sent(chunks[1], direct(1, 1)))
    earlier = natural(own_rows, other_rows, row)
    current = level_product(jnp.concatenate(chunks, axis=0), earlier, norm_scale)

    same = sent(current, direct(2, 0))
    other_near = sent(current, when_low(0, direct(2, 1)))
    other_rows = [sent(current[:DIRECT_ROWS], when_low(1, direct(2, 1))) + other_near[:DIRECT_ROWS]]
    begin = DIRECT_ROWS
    for size in RELAY_ROWS:
        ring_first = sent(current[begin:begin + size], ring_first_hop)
        other_rows.append(sent(ring_first, ring_first_exit) + other_near[begin:begin + size])
        begin += size
    current = level_product(current, natural([same], other_rows, row), norm_scale)
    return current[None]


def solution(mesh):
    return jax.shard_map(
        shards,
        mesh=mesh,
        in_specs=(P("tm", "row", None), P(), P(), P("tm", None), P("tm", None)),
        out_specs=P("tm", "row", None),
        check_vma=False,
    )
```

```python
import math

import jax
import jax.numpy as jnp
from jax import lax
from jax.sharding import PartitionSpec as P

LEVELS = 2
DIRECT_ROWS = 256
RELAY_ROWS = (384, 384)


def sent(value, route):
    tm_count = lax.axis_size("tm")
    row_count = lax.axis_size("row")
    pairs = []
    for t in range(tm_count):
        for r in range(row_count):
            target = route(t, r, tm_count, row_count)
            if target is not None:
                pairs.append((t * row_count + r, target[0] * row_count + target[1]))
    return lax.ppermute(value, ("tm", "row"), pairs)


def y_low(t):
    return (t // 2) % 2


def direct(distance, row_offset):
    return lambda t, r, n, m: ((t + distance) % n, (r + row_offset) % m)


def ring_of(t):
    return (t // 4) % 4


def ring_first_hop(t, r, n, m):
    if y_low(t) != 1:
        return None
    if ring_of(t) == 3:
        return ((t - 12) % n, r)
    return ((t + 4) % n, r)


def ring_first_exit(t, r, n, m):
    if y_low(t) != 1:
        return None
    if ring_of(t) == 0:
        return ((t + 14) % n, 1 - r)
    return ((t - 2) % n, 1 - r)


def when_low(low, route):
    return lambda t, r, n, m: route(t, r, n, m) if y_low(t) == low else None


def natural(own_rows, other_rows, row):
    return jnp.where(
        row == 0,
        jnp.concatenate(own_rows + other_rows, axis=0),
        jnp.concatenate(other_rows + own_rows, axis=0),
    )


def level_product(later, earlier, norm_scale):
    total = jnp.dot(later, earlier, preferred_element_type=jnp.float32)
    return (total * norm_scale).astype(jnp.bfloat16)


def shards(slice_ops, base_op, load_table, phase_idx, step_counts):
    state_size = base_op.shape[0]
    norm_scale = 1.0 / math.sqrt(state_size)
    phase_count = load_table.shape[0]
    row_count = lax.axis_size("row")
    half = slice_ops.shape[1]
    row = lax.axis_index("row")
    index_row = phase_idx[0]
    count_row = step_counts[0].astype(jnp.float32)
    one_hot = (
        index_row[:, None] == lax.broadcasted_iota(jnp.int32, (index_row.shape[0], phase_count), 1)
    ).astype(jnp.float32)
    table_rows = jnp.dot(one_hot, load_table, precision=lax.Precision.HIGHEST)
    gain_rows = jnp.exp(0.1 * count_row[:, None] * table_rows)
    right_factor = (base_op * gain_rows[0]).astype(jnp.bfloat16)
    left_factor = (slice_ops[0] * gain_rows[1]).astype(jnp.bfloat16)
    chunk_rows = half // 2
    chunks = []
    for c in range(2):
        product = jnp.dot(left_factor[c * chunk_rows:(c + 1) * chunk_rows], right_factor,
                          preferred_element_type=jnp.float32)
        chunks.append((product * norm_scale).astype(jnp.bfloat16))

    boundary = lambda t, r, n, m: ((t - 12) % n, r) if ring_of(t) == 3 and t % 4 == 3 else None
    boundary_exit = lambda t, r, n, m: ((t + 13) % n, r) if ring_of(t) == 0 and t % 4 == 3 else None
    not_boundary = lambda t, r, n, m: None if ring_of(t) == 3 and t % 4 == 3 else ((t + 1) % n, r)
    own_rows = [sent(chunks[0], direct(1, 0))]
    other_rows = [sent(chunks[0], direct(1, 1))]
    own_rows.append(sent(chunks[1], not_boundary) + sent(sent(chunks[1], boundary), boundary_exit))
    other_rows.append(sent(chunks[1], direct(1, 1)))
    earlier = natural(own_rows, other_rows, row)
    current = level_product(jnp.concatenate(chunks, axis=0), earlier, norm_scale)

    same = sent(current, direct(2, 0))
    other_near = sent(current, when_low(0, direct(2, 1)))
    other_rows = [sent(current[:DIRECT_ROWS], when_low(1, direct(2, 1))) + other_near[:DIRECT_ROWS]]
    begin = DIRECT_ROWS
    for size in RELAY_ROWS:
        ring_first = sent(current[begin:begin + size], ring_first_hop)
        other_rows.append(sent(ring_first, ring_first_exit) + other_near[begin:begin + size])
        begin += size
    current = level_product(current, natural([same], other_rows, row), norm_scale)
    return current[None]


def solution(mesh):
    return jax.shard_map(
        shards,
        mesh=mesh,
        in_specs=(P("tm", "row", None), P(), P(), P("tm", None), P("tm", None)),
        out_specs=P("tm", "row", None),
        check_vma=False,
    )
```

```python
import math

import jax
import jax.numpy as jnp
from jax import lax
from jax.sharding import PartitionSpec as P

LEVELS = 2
DIRECT_ROWS = 304
RELAY_ROWS = (368, 352)


def sent(value, route):
    tm_count = lax.axis_size("tm")
    row_count = lax.axis_size("row")
    pairs = []
    for t in range(tm_count):
        for r in range(row_count):
            target = route(t, r, tm_count, row_count)
            if target is not None:
                pairs.append((t * row_count + r, target[0] * row_count + target[1]))
    return lax.ppermute(value, ("tm", "row"), pairs)


def y_low(t):
    return (t // 2) % 2


def direct(distance, row_offset):
    return lambda t, r, n, m: ((t + distance) % n, (r + row_offset) % m)


def ring_of(t):
    return (t // 4) % 4


def ring_first_hop(t, r, n, m):
    if y_low(t) != 1:
        return None
    if ring_of(t) == 3:
        return ((t - 12) % n, r)
    return ((t + 4) % n, r)


def ring_first_exit(t, r, n, m):
    if y_low(t) != 1:
        return None
    if ring_of(t) == 0:
        return ((t + 14) % n, 1 - r)
    return ((t - 2) % n, 1 - r)


def when_low(low, route):
    return lambda t, r, n, m: route(t, r, n, m) if y_low(t) == low else None


def natural(own_rows, other_rows, row):
    return jnp.where(
        row == 0,
        jnp.concatenate(own_rows + other_rows, axis=0),
        jnp.concatenate(other_rows + own_rows, axis=0),
    )


def level_product(later, earlier, norm_scale):
    total = jnp.dot(later, earlier, preferred_element_type=jnp.float32)
    return (total * norm_scale).astype(jnp.bfloat16)


def shards(slice_ops, base_op, load_table, phase_idx, step_counts):
    state_size = base_op.shape[0]
    norm_scale = 1.0 / math.sqrt(state_size)
    phase_count = load_table.shape[0]
    row_count = lax.axis_size("row")
    half = slice_ops.shape[1]
    row = lax.axis_index("row")
    index_row = phase_idx[0]
    count_row = step_counts[0].astype(jnp.float32)
    one_hot = (
        index_row[:, None] == lax.broadcasted_iota(jnp.int32, (index_row.shape[0], phase_count), 1)
    ).astype(jnp.float32)
    table_rows = jnp.dot(one_hot, load_table, precision=lax.Precision.HIGHEST)
    gain_rows = jnp.exp(0.1 * count_row[:, None] * table_rows)
    right_factor = (base_op * gain_rows[0]).astype(jnp.bfloat16)
    left_factor = (slice_ops[0] * gain_rows[1]).astype(jnp.bfloat16)
    chunk_rows = half // 2
    chunks = []
    for c in range(2):
        product = jnp.dot(left_factor[c * chunk_rows:(c + 1) * chunk_rows], right_factor,
                          preferred_element_type=jnp.float32)
        chunks.append((product * norm_scale).astype(jnp.bfloat16))

    boundary_exit = lambda t, r, n, m: ((t + 13) % n, r) if ring_of(t) == 0 and t % 4 == 3 else None
    not_boundary = lambda t, r, n, m: None if ring_of(t) == 3 and t % 4 == 3 else ((t + 1) % n, r)
    own_rows = [sent(chunks[0], direct(1, 0))]
    other_rows = [sent(chunks[0], direct(1, 1))]
    crossing = lambda t, r, n, m: (((t - 12) if ring_of(t) == 3 else (t + 4)) % n, r) if t % 4 == 3 else None
    handed = lambda t, r, n, m: ((((t + 13) if ring_of(t) == 0 else (t - 3)) % n), 1 - r) if t % 4 == 3 else None
    not_cross = lambda t, r, n, m: None if t % 4 == 3 else ((t + 1) % n, 1 - r)
    crossed = sent(chunks[1], crossing)
    own_rows.append(sent(chunks[1], not_boundary) + sent(crossed, boundary_exit))
    other_rows.append(sent(chunks[1], not_cross) + sent(crossed, handed))
    earlier = natural(own_rows, other_rows, row)
    current = level_product(jnp.concatenate(chunks, axis=0), earlier, norm_scale)

    same = sent(current, direct(2, 0))
    other_near = sent(current, when_low(0, direct(2, 1)))
    other_rows = [sent(current[:DIRECT_ROWS], when_low(1, direct(2, 1))) + other_near[:DIRECT_ROWS]]
    begin = DIRECT_ROWS
    for size in RELAY_ROWS:
        ring_first = sent(current[begin:begin + size], ring_first_hop)
        other_rows.append(sent(ring_first, ring_first_exit) + other_near[begin:begin + size])
        begin += size
    current = level_product(current, natural([same], other_rows, row), norm_scale)
    return current[None]


def solution(mesh):
    return jax.shard_map(
        shards,
        mesh=mesh,
        in_specs=(P("tm", "row", None), P(), P(), P("tm", None), P("tm", None)),
        out_specs=P("tm", "row", None),
        check_vma=False,
    )
```

```python
import math

import jax
import jax.numpy as jnp
from jax import lax
from jax.sharding import PartitionSpec as P

LEVELS = 2
DIRECT_ROWS = 304
RELAY_ROWS = (368, 352)


def sent(value, route):
    tm_count = lax.axis_size("tm")
    row_count = lax.axis_size("row")
    pairs = []
    for t in range(tm_count):
        for r in range(row_count):
            target = route(t, r, tm_count, row_count)
            if target is not None:
                pairs.append((t * row_count + r, target[0] * row_count + target[1]))
    return lax.ppermute(value, ("tm", "row"), pairs)


def y_low(t):
    return (t // 2) % 2


def direct(distance, row_offset):
    return lambda t, r, n, m: ((t + distance) % n, (r + row_offset) % m)


def ring_of(t):
    return (t // 4) % 4


def ring_first_hop(t, r, n, m):
    if y_low(t) != 1:
        return None
    if ring_of(t) == 3:
        return ((t - 12) % n, r)
    return ((t + 4) % n, r)


def ring_first_exit(t, r, n, m):
    if y_low(t) != 1:
        return None
    if ring_of(t) == 0:
        return ((t + 14) % n, 1 - r)
    return ((t - 2) % n, 1 - r)


def when_low(low, route):
    return lambda t, r, n, m: route(t, r, n, m) if y_low(t) == low else None


def natural(own_rows, other_rows, row):
    return jnp.where(
        row == 0,
        jnp.concatenate(own_rows + other_rows, axis=0),
        jnp.concatenate(other_rows + own_rows, axis=0),
    )


def level_product(later, earlier, norm_scale):
    total = jnp.dot(later, earlier, preferred_element_type=jnp.float32)
    return (total * norm_scale).astype(jnp.bfloat16)


def shards(slice_ops, base_op, load_table, phase_idx, step_counts):
    state_size = base_op.shape[0]
    norm_scale = 1.0 / math.sqrt(state_size)
    phase_count = load_table.shape[0]
    row_count = lax.axis_size("row")
    half = slice_ops.shape[1]
    row = lax.axis_index("row")
    index_row = phase_idx[0]
    count_row = step_counts[0].astype(jnp.float32)
    one_hot = (
        index_row[:, None] == lax.broadcasted_iota(jnp.int32, (index_row.shape[0], phase_count), 1)
    ).astype(jnp.float32)
    table_rows = jnp.dot(one_hot, load_table, precision=lax.Precision.HIGHEST)
    gain_rows = jnp.exp(0.1 * count_row[:, None] * table_rows)
    right_factor = (base_op * gain_rows[0]).astype(jnp.bfloat16)
    left_factor = (slice_ops[0] * gain_rows[1]).astype(jnp.bfloat16)
    chunk_rows = half // 2
    chunks = []
    for c in range(2):
        product = jnp.dot(left_factor[c * chunk_rows:(c + 1) * chunk_rows], right_factor,
                          preferred_element_type=jnp.float32)
        chunks.append((product * norm_scale).astype(jnp.bfloat16))

    own_rows = [sent(chunks[0], direct(1, 0))]
    other_rows = [sent(chunks[0], direct(1, 1))]
    crossing = lambda t, r, n, m: (((t - 12) if ring_of(t) == 3 else (t + 4)) % n, r) if t % 4 == 3 else None
    handed = lambda t, r, n, m: ((((t + 13) if ring_of(t) == 0 else (t - 3)) % n), 1 - r) if t % 4 == 3 else None
    not_cross = lambda t, r, n, m: None if t % 4 == 3 else ((t + 1) % n, 1 - r)
    crossed = sent(chunks[1], crossing)
    handed_same = lambda t, r, n, m: ((((t + 13) if ring_of(t) == 0 else (t - 3)) % n), r) if t % 4 == 3 else None
    same_not_cross = lambda t, r, n, m: None if t % 4 == 3 else ((t + 1) % n, r)
    own_rows.append(sent(chunks[1], same_not_cross) + sent(crossed, handed_same))
    other_rows.append(sent(chunks[1], not_cross) + sent(crossed, handed))
    earlier = natural(own_rows, other_rows, row)
    current = level_product(jnp.concatenate(chunks, axis=0), earlier, norm_scale)

    same = sent(current, direct(2, 0))
    other_near = sent(current, when_low(0, direct(2, 1)))
    other_rows = [sent(current[:DIRECT_ROWS], when_low(1, direct(2, 1))) + other_near[:DIRECT_ROWS]]
    begin = DIRECT_ROWS
    for size in RELAY_ROWS:
        ring_first = sent(current[begin:begin + size], ring_first_hop)
        other_rows.append(sent(ring_first, ring_first_exit) + other_near[begin:begin + size])
        begin += size
    current = level_product(current, natural([same], other_rows, row), norm_scale)
    return current[None]


def solution(mesh):
    return jax.shard_map(
        shards,
        mesh=mesh,
        in_specs=(P("tm", "row", None), P(), P(), P("tm", None), P("tm", None)),
        out_specs=P("tm", "row", None),
        check_vma=False,
    )
```

```python
import math

import jax
import jax.numpy as jnp
from jax import lax
from jax.sharding import PartitionSpec as P

LEVELS = 2
DIRECT_ROWS = 208
RELAY_ROWS = (416, 400)


def sent(value, route):
    tm_count = lax.axis_size("tm")
    row_count = lax.axis_size("row")
    pairs = []
    for t in range(tm_count):
        for r in range(row_count):
            target = route(t, r, tm_count, row_count)
            if target is not None:
                pairs.append((t * row_count + r, target[0] * row_count + target[1]))
    return lax.ppermute(value, ("tm", "row"), pairs)


def y_low(t):
    return (t // 2) % 2


def direct(distance, row_offset):
    return lambda t, r, n, m: ((t + distance) % n, (r + row_offset) % m)


def ring_of(t):
    return (t // 4) % 4


def ring_first_hop(t, r, n, m):
    if y_low(t) != 1:
        return None
    if ring_of(t) == 3:
        return ((t - 12) % n, r)
    return ((t + 4) % n, r)


def ring_first_exit(t, r, n, m):
    if y_low(t) != 1:
        return None
    if ring_of(t) == 0:
        return ((t + 14) % n, 1 - r)
    return ((t - 2) % n, 1 - r)


def when_low(low, route):
    return lambda t, r, n, m: route(t, r, n, m) if y_low(t) == low else None


def natural(own_rows, other_rows, row):
    return jnp.where(
        row == 0,
        jnp.concatenate(own_rows + other_rows, axis=0),
        jnp.concatenate(other_rows + own_rows, axis=0),
    )


def level_product(later, earlier, norm_scale):
    total = jnp.dot(later, earlier, preferred_element_type=jnp.float32)
    return (total * norm_scale).astype(jnp.bfloat16)


def shards(slice_ops, base_op, load_table, phase_idx, step_counts):
    state_size = base_op.shape[0]
    norm_scale = 1.0 / math.sqrt(state_size)
    phase_count = load_table.shape[0]
    row_count = lax.axis_size("row")
    half = slice_ops.shape[1]
    row = lax.axis_index("row")
    index_row = phase_idx[0]
    count_row = step_counts[0].astype(jnp.float32)
    one_hot = (
        index_row[:, None] == lax.broadcasted_iota(jnp.int32, (index_row.shape[0], phase_count), 1)
    ).astype(jnp.float32)
    table_rows = jnp.dot(one_hot, load_table, precision=lax.Precision.HIGHEST)
    gain_rows = jnp.exp(0.1 * count_row[:, None] * table_rows)
    right_factor = (base_op * gain_rows[0]).astype(jnp.bfloat16)
    left_factor = (slice_ops[0] * gain_rows[1]).astype(jnp.bfloat16)
    chunk_rows = half // 2
    chunks = []
    for c in range(2):
        product = jnp.dot(left_factor[c * chunk_rows:(c + 1) * chunk_rows], right_factor,
                          preferred_element_type=jnp.float32)
        chunks.append((product * norm_scale).astype(jnp.bfloat16))

    boundary = lambda t, r, n, m: ((t - 12) % n, r) if ring_of(t) == 3 and t % 4 == 3 else None
    boundary_exit = lambda t, r, n, m: ((t + 13) % n, r) if ring_of(t) == 0 and t % 4 == 3 else None
    not_boundary = lambda t, r, n, m: None if ring_of(t) == 3 and t % 4 == 3 else ((t + 1) % n, r)
    own_rows = [sent(chunks[0], direct(1, 0))]
    other_rows = [sent(chunks[0], direct(1, 1))]
    own_rows.append(sent(chunks[1], not_boundary) + sent(sent(chunks[1], boundary), boundary_exit))
    other_rows.append(sent(chunks[1], direct(1, 1)))
    earlier = natural(own_rows, other_rows, row)
    current = level_product(jnp.concatenate(chunks, axis=0), earlier, norm_scale)

    same = sent(current, direct(2, 0))
    other_near = sent(current, when_low(0, direct(2, 1)))
    other_rows = [sent(current[:DIRECT_ROWS], when_low(1, direct(2, 1))) + other_near[:DIRECT_ROWS]]
    begin = DIRECT_ROWS
    previous = None
    for size in RELAY_ROWS:
        piece = current[begin:begin + size]
        if previous is not None:
            piece, _ = lax.optimization_barrier((piece, previous))
        ring_first = sent(piece, ring_first_hop)
        previous = ring_first
        other_rows.append(sent(ring_first, ring_first_exit) + other_near[begin:begin + size])
        begin += size
    current = level_product(current, natural([same], other_rows, row), norm_scale)
    return current[None]


def solution(mesh):
    return jax.shard_map(
        shards,
        mesh=mesh,
        in_specs=(P("tm", "row", None), P(), P(), P("tm", None), P("tm", None)),
        out_specs=P("tm", "row", None),
        check_vma=False,
    )
```

```python
import math

import jax
import jax.numpy as jnp
from jax import lax
from jax.sharding import PartitionSpec as P

LEVELS = 2
DIRECT_ROWS = 304
RELAY_ROWS = (368, 352)


def sent(value, route):
    tm_count = lax.axis_size("tm")
    row_count = lax.axis_size("row")
    pairs = []
    for t in range(tm_count):
        for r in range(row_count):
            target = route(t, r, tm_count, row_count)
            if target is not None:
                pairs.append((t * row_count + r, target[0] * row_count + target[1]))
    return lax.ppermute(value, ("tm", "row"), pairs)


def y_low(t):
    return (t // 2) % 2


def direct(distance, row_offset):
    return lambda t, r, n, m: ((t + distance) % n, (r + row_offset) % m)


def ring_of(t):
    return (t // 4) % 4


def ring_first_hop(t, r, n, m):
    if y_low(t) != 1:
        return None
    if ring_of(t) == 3:
        return ((t - 12) % n, r)
    return ((t + 4) % n, r)


def ring_first_exit(t, r, n, m):
    if y_low(t) != 1:
        return None
    if ring_of(t) == 0:
        return ((t + 14) % n, 1 - r)
    return ((t - 2) % n, 1 - r)


def when_low(low, route):
    return lambda t, r, n, m: route(t, r, n, m) if y_low(t) == low else None


def natural(own_rows, other_rows, row):
    return jnp.where(
        row == 0,
        jnp.concatenate(own_rows + other_rows, axis=0),
        jnp.concatenate(other_rows + own_rows, axis=0),
    )


def level_product(later, earlier, norm_scale):
    total = jnp.dot(later, earlier, preferred_element_type=jnp.float32)
    return (total * norm_scale).astype(jnp.bfloat16)


def shards(slice_ops, base_op, load_table, phase_idx, step_counts):
    state_size = base_op.shape[0]
    norm_scale = 1.0 / math.sqrt(state_size)
    phase_count = load_table.shape[0]
    row_count = lax.axis_size("row")
    half = slice_ops.shape[1]
    row = lax.axis_index("row")
    index_row = phase_idx[0]
    count_row = step_counts[0].astype(jnp.float32)
    one_hot = (
        index_row[:, None] == lax.broadcasted_iota(jnp.int32, (index_row.shape[0], phase_count), 1)
    ).astype(jnp.float32)
    table_rows = jnp.dot(one_hot, load_table, precision=lax.Precision.HIGHEST)
    gain_rows = jnp.exp(0.1 * count_row[:, None] * table_rows)
    right_factor = (base_op * gain_rows[0]).astype(jnp.bfloat16)
    left_factor = (slice_ops[0] * gain_rows[1]).astype(jnp.bfloat16)
    first_rows = half * 3 // 8
    bounds = ((0, first_rows), (first_rows, half))
    chunks = []
    for begin, end in bounds:
        product = jnp.dot(left_factor[begin:end], right_factor,
                          preferred_element_type=jnp.float32)
        chunks.append((product * norm_scale).astype(jnp.bfloat16))

    boundary = lambda t, r, n, m: ((t - 12) % n, r) if ring_of(t) == 3 and t % 4 == 3 else None
    boundary_exit = lambda t, r, n, m: ((t + 13) % n, r) if ring_of(t) == 0 and t % 4 == 3 else None
    not_boundary = lambda t, r, n, m: None if ring_of(t) == 3 and t % 4 == 3 else ((t + 1) % n, r)
    own_rows = [sent(chunks[0], direct(1, 0))]
    other_rows = [sent(chunks[0], direct(1, 1))]
    own_rows.append(sent(chunks[1], not_boundary) + sent(sent(chunks[1], boundary), boundary_exit))
    other_rows.append(sent(chunks[1], direct(1, 1)))
    earlier = natural(own_rows, other_rows, row)
    current = level_product(jnp.concatenate(chunks, axis=0), earlier, norm_scale)

    same = sent(current, direct(2, 0))
    other_near = sent(current, when_low(0, direct(2, 1)))
    other_rows = [sent(current[:DIRECT_ROWS], when_low(1, direct(2, 1))) + other_near[:DIRECT_ROWS]]
    begin = DIRECT_ROWS
    for size in RELAY_ROWS:
        ring_first = sent(current[begin:begin + size], ring_first_hop)
        other_rows.append(sent(ring_first, ring_first_exit) + other_near[begin:begin + size])
        begin += size
    current = level_product(current, natural([same], other_rows, row), norm_scale)
    return current[None]


def solution(mesh):
    return jax.shard_map(
        shards,
        mesh=mesh,
        in_specs=(P("tm", "row", None), P(), P(), P("tm", None), P("tm", None)),
        out_specs=P("tm", "row", None),
        check_vma=False,
    )
```

```python
import math

import jax
import jax.numpy as jnp
from jax import lax
from jax.sharding import PartitionSpec as P

LEVELS = 2
DIRECT_ROWS = 304
RELAY_ROWS = (368, 352)


def sent(value, route):
    tm_count = lax.axis_size("tm")
    row_count = lax.axis_size("row")
    pairs = []
    for t in range(tm_count):
        for r in range(row_count):
            target = route(t, r, tm_count, row_count)
            if target is not None:
                pairs.append((t * row_count + r, target[0] * row_count + target[1]))
    return lax.ppermute(value, ("tm", "row"), pairs)


def y_low(t):
    return (t // 2) % 2


def direct(distance, row_offset):
    return lambda t, r, n, m: ((t + distance) % n, (r + row_offset) % m)


def ring_of(t):
    return (t // 4) % 4


def ring_first_hop(t, r, n, m):
    if y_low(t) != 1:
        return None
    if ring_of(t) == 3:
        return ((t - 12) % n, r)
    return ((t + 4) % n, r)


def ring_first_exit(t, r, n, m):
    if y_low(t) != 1:
        return None
    if ring_of(t) == 0:
        return ((t + 14) % n, 1 - r)
    return ((t - 2) % n, 1 - r)


def when_low(low, route):
    return lambda t, r, n, m: route(t, r, n, m) if y_low(t) == low else None


def natural(own_rows, other_rows, row):
    return jnp.where(
        row == 0,
        jnp.concatenate(own_rows + other_rows, axis=0),
        jnp.concatenate(other_rows + own_rows, axis=0),
    )


def level_product(later, earlier, norm_scale):
    total = jnp.dot(later, earlier, preferred_element_type=jnp.float32)
    return (total * norm_scale).astype(jnp.bfloat16)


def shards(slice_ops, base_op, load_table, phase_idx, step_counts):
    state_size = base_op.shape[0]
    norm_scale = 1.0 / math.sqrt(state_size)
    phase_count = load_table.shape[0]
    row_count = lax.axis_size("row")
    half = slice_ops.shape[1]
    row = lax.axis_index("row")
    index_row = phase_idx[0]
    count_row = step_counts[0].astype(jnp.float32)
    one_hot = (
        index_row[:, None] == lax.broadcasted_iota(jnp.int32, (index_row.shape[0], phase_count), 1)
    ).astype(jnp.float32)
    table_rows = jnp.dot(one_hot, load_table, precision=lax.Precision.HIGHEST)
    gain_rows = jnp.exp(0.1 * count_row[:, None] * table_rows)
    right_factor = (base_op * gain_rows[0]).astype(jnp.bfloat16)
    left_factor = (slice_ops[0] * gain_rows[1]).astype(jnp.bfloat16)
    chunk_rows = half // 2
    chunks = []
    for c in range(2):
        product = jnp.dot(left_factor[c * chunk_rows:(c + 1) * chunk_rows], right_factor,
                          preferred_element_type=jnp.float32)
        chunks.append((product * norm_scale).astype(jnp.bfloat16))

    own_rows = [sent(chunks[0], direct(1, 0))]
    other_rows = [sent(chunks[0], direct(1, 1))]
    own_rows.append(sent(chunks[1], direct(1, 0)))
    other_rows.append(sent(chunks[1], direct(1, 1)))
    earlier = natural(own_rows, other_rows, row)
    current = level_product(jnp.concatenate(chunks, axis=0), earlier, norm_scale)

    same = sent(current, direct(2, 0))
    other_near = sent(current, when_low(0, direct(2, 1)))
    other_rows = [sent(current[:DIRECT_ROWS], when_low(1, direct(2, 1))) + other_near[:DIRECT_ROWS]]
    begin = DIRECT_ROWS
    for size in RELAY_ROWS:
        ring_first = sent(current[begin:begin + size], ring_first_hop)
        other_rows.append(sent(ring_first, ring_first_exit) + other_near[begin:begin + size])
        begin += size
    current = level_product(current, natural([same], other_rows, row), norm_scale)
    return current[None]


def solution(mesh):
    return jax.shard_map(
        shards,
        mesh=mesh,
        in_specs=(P("tm", "row", None), P(), P(), P("tm", None), P("tm", None)),
        out_specs=P("tm", "row", None),
        check_vma=False,
    )
```

```python
import math

import jax
import jax.numpy as jnp
from jax import lax
from jax.sharding import PartitionSpec as P

LEVELS = 2
DIRECT_ROWS = 352
RELAY_ROWS = (672,)


def sent(value, route):
    tm_count = lax.axis_size("tm")
    row_count = lax.axis_size("row")
    pairs = []
    for t in range(tm_count):
        for r in range(row_count):
            target = route(t, r, tm_count, row_count)
            if target is not None:
                pairs.append((t * row_count + r, target[0] * row_count + target[1]))
    return lax.ppermute(value, ("tm", "row"), pairs)


def y_low(t):
    return (t // 2) % 2


def direct(distance, row_offset):
    return lambda t, r, n, m: ((t + distance) % n, (r + row_offset) % m)


def ring_of(t):
    return (t // 4) % 4


def ring_first_hop(t, r, n, m):
    if y_low(t) != 1:
        return None
    if ring_of(t) == 3:
        return ((t - 12) % n, r)
    return ((t + 4) % n, r)


def ring_first_exit(t, r, n, m):
    if y_low(t) != 1:
        return None
    if ring_of(t) == 0:
        return ((t + 14) % n, 1 - r)
    return ((t - 2) % n, 1 - r)


def when_low(low, route):
    return lambda t, r, n, m: route(t, r, n, m) if y_low(t) == low else None


def natural(own_rows, other_rows, row):
    return jnp.where(
        row == 0,
        jnp.concatenate(own_rows + other_rows, axis=0),
        jnp.concatenate(other_rows + own_rows, axis=0),
    )


def level_product(later, earlier, norm_scale):
    total = jnp.dot(later, earlier, preferred_element_type=jnp.float32)
    return (total * norm_scale).astype(jnp.bfloat16)


def shards(slice_ops, base_op, load_table, phase_idx, step_counts):
    state_size = base_op.shape[0]
    norm_scale = 1.0 / math.sqrt(state_size)
    phase_count = load_table.shape[0]
    row_count = lax.axis_size("row")
    half = slice_ops.shape[1]
    row = lax.axis_index("row")
    index_row = phase_idx[0]
    count_row = step_counts[0].astype(jnp.float32)
    one_hot = (
        index_row[:, None] == lax.broadcasted_iota(jnp.int32, (index_row.shape[0], phase_count), 1)
    ).astype(jnp.float32)
    table_rows = jnp.dot(one_hot, load_table, precision=lax.Precision.HIGHEST)
    gain_rows = jnp.exp(0.1 * count_row[:, None] * table_rows)
    right_factor = (base_op * gain_rows[0]).astype(jnp.bfloat16)
    left_factor = (slice_ops[0] * gain_rows[1]).astype(jnp.bfloat16)
    chunk_rows = half // 2
    chunks = []
    for c in range(2):
        product = jnp.dot(left_factor[c * chunk_rows:(c + 1) * chunk_rows], right_factor,
                          preferred_element_type=jnp.float32)
        chunks.append((product * norm_scale).astype(jnp.bfloat16))

    own_rows = [sent(chunks[0], direct(1, 0))]
    other_rows = [sent(chunks[0], direct(1, 1))]
    own_rows.append(sent(chunks[1], direct(1, 0)))
    other_rows.append(sent(chunks[1], direct(1, 1)))
    earlier = natural(own_rows, other_rows, row)
    current = level_product(jnp.concatenate(chunks, axis=0), earlier, norm_scale)

    same = sent(current, direct(2, 0))
    other_near = sent(current, when_low(0, direct(2, 1)))
    other_rows = [sent(current[:DIRECT_ROWS], when_low(1, direct(2, 1))) + other_near[:DIRECT_ROWS]]
    begin = DIRECT_ROWS
    for size in RELAY_ROWS:
        ring_first = sent(current[begin:begin + size], ring_first_hop)
        other_rows.append(sent(ring_first, ring_first_exit) + other_near[begin:begin + size])
        begin += size
    current = level_product(current, natural([same], other_rows, row), norm_scale)
    return current[None]


def solution(mesh):
    return jax.shard_map(
        shards,
        mesh=mesh,
        in_specs=(P("tm", "row", None), P(), P(), P("tm", None), P("tm", None)),
        out_specs=P("tm", "row", None),
        check_vma=False,
    )
```

```python
import math

import jax
import jax.numpy as jnp
from jax import lax
from jax.sharding import PartitionSpec as P

LEVELS = 2
DIRECT_ROWS = 336
RELAY_ROWS = (352, 336)


def sent(value, route):
    tm_count = lax.axis_size("tm")
    row_count = lax.axis_size("row")
    pairs = []
    for t in range(tm_count):
        for r in range(row_count):
            target = route(t, r, tm_count, row_count)
            if target is not None:
                pairs.append((t * row_count + r, target[0] * row_count + target[1]))
    return lax.ppermute(value, ("tm", "row"), pairs)


def y_low(t):
    return (t // 2) % 2


def direct(distance, row_offset):
    return lambda t, r, n, m: ((t + distance) % n, (r + row_offset) % m)


def ring_of(t):
    return (t // 4) % 4


def ring_first_hop(t, r, n, m):
    if y_low(t) != 1:
        return None
    if ring_of(t) == 3:
        return ((t - 12) % n, r)
    return ((t + 4) % n, r)


def ring_first_exit(t, r, n, m):
    if y_low(t) != 1:
        return None
    if ring_of(t) == 0:
        return ((t + 14) % n, 1 - r)
    return ((t - 2) % n, 1 - r)


def when_low(low, route):
    return lambda t, r, n, m: route(t, r, n, m) if y_low(t) == low else None


def natural(own_rows, other_rows, row):
    return jnp.where(
        row == 0,
        jnp.concatenate(own_rows + other_rows, axis=0),
        jnp.concatenate(other_rows + own_rows, axis=0),
    )


def level_product(later, earlier, norm_scale):
    total = jnp.dot(later, earlier, preferred_element_type=jnp.float32)
    return (total * norm_scale).astype(jnp.bfloat16)


def shards(slice_ops, base_op, load_table, phase_idx, step_counts):
    state_size = base_op.shape[0]
    norm_scale = 1.0 / math.sqrt(state_size)
    phase_count = load_table.shape[0]
    row_count = lax.axis_size("row")
    half = slice_ops.shape[1]
    row = lax.axis_index("row")
    index_row = phase_idx[0]
    count_row = step_counts[0].astype(jnp.float32)
    one_hot = (
        index_row[:, None] == lax.broadcasted_iota(jnp.int32, (index_row.shape[0], phase_count), 1)
    ).astype(jnp.float32)
    table_rows = jnp.dot(one_hot, load_table, precision=lax.Precision.HIGHEST)
    gain_rows = jnp.exp(0.1 * count_row[:, None] * table_rows)
    right_factor = (base_op * gain_rows[0]).astype(jnp.bfloat16)
    left_factor = (slice_ops[0] * gain_rows[1]).astype(jnp.bfloat16)
    chunk_rows = half // 2
    chunks = []
    for c in range(2):
        product = jnp.dot(left_factor[c * chunk_rows:(c + 1) * chunk_rows], right_factor,
                          preferred_element_type=jnp.float32)
        chunks.append((product * norm_scale).astype(jnp.bfloat16))

    own_rows = [sent(chunks[0], direct(1, 0))]
    other_rows = [sent(chunks[0], direct(1, 1))]
    own_rows.append(sent(chunks[1], direct(1, 0)))
    other_rows.append(sent(chunks[1], direct(1, 1)))
    earlier = natural(own_rows, other_rows, row)
    current = level_product(jnp.concatenate(chunks, axis=0), earlier, norm_scale)

    same = sent(current, direct(2, 0))
    other_near = sent(current, when_low(0, direct(2, 1)))
    other_rows = [sent(current[:DIRECT_ROWS], when_low(1, direct(2, 1))) + other_near[:DIRECT_ROWS]]
    begin = DIRECT_ROWS
    for size in RELAY_ROWS:
        ring_first = sent(current[begin:begin + size], ring_first_hop)
        other_rows.append(sent(ring_first, ring_first_exit) + other_near[begin:begin + size])
        begin += size
    current = level_product(current, natural([same], other_rows, row), norm_scale)
    return current[None]


def solution(mesh):
    return jax.shard_map(
        shards,
        mesh=mesh,
        in_specs=(P("tm", "row", None), P(), P(), P("tm", None), P("tm", None)),
        out_specs=P("tm", "row", None),
        check_vma=False,
    )
```

```python
import math

import jax
import jax.numpy as jnp
from jax import lax
from jax.sharding import PartitionSpec as P

LEVELS = 2
DIRECT_ROWS = 304
RELAY_ROWS = (352, 368)


def sent(value, route):
    tm_count = lax.axis_size("tm")
    row_count = lax.axis_size("row")
    pairs = []
    for t in range(tm_count):
        for r in range(row_count):
            target = route(t, r, tm_count, row_count)
            if target is not None:
                pairs.append((t * row_count + r, target[0] * row_count + target[1]))
    return lax.ppermute(value, ("tm", "row"), pairs)


def y_low(t):
    return (t // 2) % 2


def direct(distance, row_offset):
    return lambda t, r, n, m: ((t + distance) % n, (r + row_offset) % m)


def ring_of(t):
    return (t // 4) % 4


def ring_first_hop(t, r, n, m):
    if y_low(t) != 1:
        return None
    if ring_of(t) == 3:
        return ((t - 12) % n, r)
    return ((t + 4) % n, r)


def ring_first_exit(t, r, n, m):
    if y_low(t) != 1:
        return None
    if ring_of(t) == 0:
        return ((t + 14) % n, 1 - r)
    return ((t - 2) % n, 1 - r)


def when_low(low, route):
    return lambda t, r, n, m: route(t, r, n, m) if y_low(t) == low else None


def natural(own_rows, other_rows, row):
    return jnp.where(
        row == 0,
        jnp.concatenate(own_rows + other_rows, axis=0),
        jnp.concatenate(other_rows + own_rows, axis=0),
    )


def level_product(later, earlier, norm_scale):
    total = jnp.dot(later, earlier, preferred_element_type=jnp.float32)
    return (total * norm_scale).astype(jnp.bfloat16)


def shards(slice_ops, base_op, load_table, phase_idx, step_counts):
    state_size = base_op.shape[0]
    norm_scale = 1.0 / math.sqrt(state_size)
    phase_count = load_table.shape[0]
    row_count = lax.axis_size("row")
    half = slice_ops.shape[1]
    row = lax.axis_index("row")
    index_row = phase_idx[0]
    count_row = step_counts[0].astype(jnp.float32)
    one_hot = (
        index_row[:, None] == lax.broadcasted_iota(jnp.int32, (index_row.shape[0], phase_count), 1)
    ).astype(jnp.float32)
    table_rows = jnp.dot(one_hot, load_table, precision=lax.Precision.HIGHEST)
    gain_rows = jnp.exp(0.1 * count_row[:, None] * table_rows)
    right_factor = (base_op * gain_rows[0]).astype(jnp.bfloat16)
    left_factor = (slice_ops[0] * gain_rows[1]).astype(jnp.bfloat16)
    chunk_rows = half // 2
    chunks = []
    for c in range(2):
        product = jnp.dot(left_factor[c * chunk_rows:(c + 1) * chunk_rows], right_factor,
                          preferred_element_type=jnp.float32)
        chunks.append((product * norm_scale).astype(jnp.bfloat16))

    own_rows = [sent(chunks[0], direct(1, 0))]
    other_rows = [sent(chunks[0], direct(1, 1))]
    own_rows.append(sent(chunks[1], direct(1, 0)))
    other_rows.append(sent(chunks[1], direct(1, 1)))
    earlier = natural(own_rows, other_rows, row)
    current = level_product(jnp.concatenate(chunks, axis=0), earlier, norm_scale)

    same = sent(current, direct(2, 0))
    other_near = sent(current, when_low(0, direct(2, 1)))
    other_rows = [sent(current[:DIRECT_ROWS], when_low(1, direct(2, 1))) + other_near[:DIRECT_ROWS]]
    begin = DIRECT_ROWS
    for size in RELAY_ROWS:
        ring_first = sent(current[begin:begin + size], ring_first_hop)
        other_rows.append(sent(ring_first, ring_first_exit) + other_near[begin:begin + size])
        begin += size
    current = level_product(current, natural([same], other_rows, row), norm_scale)
    return current[None]


def solution(mesh):
    return jax.shard_map(
        shards,
        mesh=mesh,
        in_specs=(P("tm", "row", None), P(), P(), P("tm", None), P("tm", None)),
        out_specs=P("tm", "row", None),
        check_vma=False,
    )
```

```python
import math

import jax
import jax.numpy as jnp
from jax import lax
from jax.sharding import PartitionSpec as P

LEVELS = 2
DIRECT_ROWS = 304
RELAY_ROWS = (320, 400)


def sent(value, route):
    tm_count = lax.axis_size("tm")
    row_count = lax.axis_size("row")
    pairs = []
    for t in range(tm_count):
        for r in range(row_count):
            target = route(t, r, tm_count, row_count)
            if target is not None:
                pairs.append((t * row_count + r, target[0] * row_count + target[1]))
    return lax.ppermute(value, ("tm", "row"), pairs)


def y_low(t):
    return (t // 2) % 2


def direct(distance, row_offset):
    return lambda t, r, n, m: ((t + distance) % n, (r + row_offset) % m)


def ring_of(t):
    return (t // 4) % 4


def ring_first_hop(t, r, n, m):
    if y_low(t) != 1:
        return None
    if ring_of(t) == 3:
        return ((t - 12) % n, r)
    return ((t + 4) % n, r)


def ring_first_exit(t, r, n, m):
    if y_low(t) != 1:
        return None
    if ring_of(t) == 0:
        return ((t + 14) % n, 1 - r)
    return ((t - 2) % n, 1 - r)


def when_low(low, route):
    return lambda t, r, n, m: route(t, r, n, m) if y_low(t) == low else None


def natural(own_rows, other_rows, row):
    return jnp.where(
        row == 0,
        jnp.concatenate(own_rows + other_rows, axis=0),
        jnp.concatenate(other_rows + own_rows, axis=0),
    )


def level_product(later, earlier, norm_scale):
    total = jnp.dot(later, earlier, preferred_element_type=jnp.float32)
    return (total * norm_scale).astype(jnp.bfloat16)


def shards(slice_ops, base_op, load_table, phase_idx, step_counts):
    state_size = base_op.shape[0]
    norm_scale = 1.0 / math.sqrt(state_size)
    phase_count = load_table.shape[0]
    row_count = lax.axis_size("row")
    half = slice_ops.shape[1]
    row = lax.axis_index("row")
    index_row = phase_idx[0]
    count_row = step_counts[0].astype(jnp.float32)
    one_hot = (
        index_row[:, None] == lax.broadcasted_iota(jnp.int32, (index_row.shape[0], phase_count), 1)
    ).astype(jnp.float32)
    table_rows = jnp.dot(one_hot, load_table, precision=lax.Precision.HIGHEST)
    gain_rows = jnp.exp(0.1 * count_row[:, None] * table_rows)
    right_factor = (base_op * gain_rows[0]).astype(jnp.bfloat16)
    left_factor = (slice_ops[0] * gain_rows[1]).astype(jnp.bfloat16)
    chunk_rows = half // 2
    chunks = []
    for c in range(2):
        product = jnp.dot(left_factor[c * chunk_rows:(c + 1) * chunk_rows], right_factor,
                          preferred_element_type=jnp.float32)
        chunks.append((product * norm_scale).astype(jnp.bfloat16))

    own_rows = [sent(chunks[0], direct(1, 0))]
    other_rows = [sent(chunks[0], direct(1, 1))]
    own_rows.append(sent(chunks[1], direct(1, 0)))
    other_rows.append(sent(chunks[1], direct(1, 1)))
    earlier = natural(own_rows, other_rows, row)
    current = level_product(jnp.concatenate(chunks, axis=0), earlier, norm_scale)

    same = sent(current, direct(2, 0))
    other_near = sent(current, when_low(0, direct(2, 1)))
    other_rows = [sent(current[:DIRECT_ROWS], when_low(1, direct(2, 1))) + other_near[:DIRECT_ROWS]]
    begin = DIRECT_ROWS
    for size in RELAY_ROWS:
        ring_first = sent(current[begin:begin + size], ring_first_hop)
        other_rows.append(sent(ring_first, ring_first_exit) + other_near[begin:begin + size])
        begin += size
    current = level_product(current, natural([same], other_rows, row), norm_scale)
    return current[None]


def solution(mesh):
    return jax.shard_map(
        shards,
        mesh=mesh,
        in_specs=(P("tm", "row", None), P(), P(), P("tm", None), P("tm", None)),
        out_specs=P("tm", "row", None),
        check_vma=False,
    )
```

```python
import math

import jax
import jax.numpy as jnp
from jax import lax
from jax.sharding import PartitionSpec as P

LEVELS = 2
DIRECT_ROWS = 288
RELAY_ROWS = (368, 368)


def sent(value, route):
    tm_count = lax.axis_size("tm")
    row_count = lax.axis_size("row")
    pairs = []
    for t in range(tm_count):
        for r in range(row_count):
            target = route(t, r, tm_count, row_count)
            if target is not None:
                pairs.append((t * row_count + r, target[0] * row_count + target[1]))
    return lax.ppermute(value, ("tm", "row"), pairs)


def y_low(t):
    return (t // 2) % 2


def direct(distance, row_offset):
    return lambda t, r, n, m: ((t + distance) % n, (r + row_offset) % m)


def ring_of(t):
    return (t // 4) % 4


def ring_first_hop(t, r, n, m):
    if y_low(t) != 1:
        return None
    if ring_of(t) == 3:
        return ((t - 12) % n, r)
    return ((t + 4) % n, r)


def ring_first_exit(t, r, n, m):
    if y_low(t) != 1:
        return None
    if ring_of(t) == 0:
        return ((t + 14) % n, 1 - r)
    return ((t - 2) % n, 1 - r)


def when_low(low, route):
    return lambda t, r, n, m: route(t, r, n, m) if y_low(t) == low else None


def natural(own_rows, other_rows, row):
    return jnp.where(
        row == 0,
        jnp.concatenate(own_rows + other_rows, axis=0),
        jnp.concatenate(other_rows + own_rows, axis=0),
    )


def level_product(later, earlier, norm_scale):
    total = jnp.dot(later, earlier, preferred_element_type=jnp.float32)
    return (total * norm_scale).astype(jnp.bfloat16)


def shards(slice_ops, base_op, load_table, phase_idx, step_counts):
    state_size = base_op.shape[0]
    norm_scale = 1.0 / math.sqrt(state_size)
    phase_count = load_table.shape[0]
    row_count = lax.axis_size("row")
    half = slice_ops.shape[1]
    row = lax.axis_index("row")
    index_row = phase_idx[0]
    count_row = step_counts[0].astype(jnp.float32)
    one_hot = (
        index_row[:, None] == lax.broadcasted_iota(jnp.int32, (index_row.shape[0], phase_count), 1)
    ).astype(jnp.float32)
    table_rows = jnp.dot(one_hot, load_table, precision=lax.Precision.HIGHEST)
    gain_rows = jnp.exp(0.1 * count_row[:, None] * table_rows)
    right_factor = (base_op * gain_rows[0]).astype(jnp.bfloat16)
    left_factor = (slice_ops[0] * gain_rows[1]).astype(jnp.bfloat16)
    chunk_rows = half // 2
    chunks = []
    for c in range(2):
        product = jnp.dot(left_factor[c * chunk_rows:(c + 1) * chunk_rows], right_factor,
                          preferred_element_type=jnp.float32)
        chunks.append((product * norm_scale).astype(jnp.bfloat16))

    own_rows = [sent(chunks[0], direct(1, 0))]
    other_rows = [sent(chunks[0], direct(1, 1))]
    own_rows.append(sent(chunks[1], direct(1, 0)))
    other_rows.append(sent(chunks[1], direct(1, 1)))
    earlier = natural(own_rows, other_rows, row)
    current = level_product(jnp.concatenate(chunks, axis=0), earlier, norm_scale)

    same = sent(current, direct(2, 0))
    other_near = sent(current, when_low(0, direct(2, 1)))
    other_rows = [sent(current[:DIRECT_ROWS], when_low(1, direct(2, 1))) + other_near[:DIRECT_ROWS]]
    begin = DIRECT_ROWS
    for size in RELAY_ROWS:
        ring_first = sent(current[begin:begin + size], ring_first_hop)
        other_rows.append(sent(ring_first, ring_first_exit) + other_near[begin:begin + size])
        begin += size
    current = level_product(current, natural([same], other_rows, row), norm_scale)
    return current[None]


def solution(mesh):
    return jax.shard_map(
        shards,
        mesh=mesh,
        in_specs=(P("tm", "row", None), P(), P(), P("tm", None), P("tm", None)),
        out_specs=P("tm", "row", None),
        check_vma=False,
    )
```
